256 devices in a mesh: lon: 16 (over x_lo, z), lat: 16 (over y, x_hi, core).
Axes of the slice: x: 4 (x_hi: 2, x_lo: 2; x = x_hi * 2 + x_lo), y: 4, z: 8, core: 2. Of those that a mesh axis runs over, the one named last changes fastest.
Arguments:
- state: float32 [4, 4, 512, 4096], P(None, None, 'lat', 'lon'), may hold values from -3 to 3
- cotangent: float32 [4, 4, 512, 4096], P(None, None, 'lat', 'lon'), may hold values from -6 to 6
- seamask: int32 [512, 4096], P('lat', 'lon'), may hold values 0 or 1
- levels: int32 [512, 4096], P('lat', 'lon'), may hold values from 1 to 4
Outputs:
- final_state: float32 [4, 4, 512, 4096], P(None, None, 'lat', 'lon')
- adjoint_state: float32 [4, 4, 512, 4096], P(None, None, 'lat', 'lon')
The draws below stay inside these ranges and needn't reach their ends.
All inputs are finite; a program needn't handle non-finite values. No bound on the sum of `seamask` on one device may be relied on, other than what follows from the above.
Results may differ from the reference program's by a relative error of at most 0.0003.
Values sent between devices are 32-bit elements; how exact they have to be, the bound alone decides.
No kernel may reach another device: no remote copies, remote signals or barrier semaphores. Data moves between devices by JAX's collectives and lax.ppermute only.
A program may use at most 64 MiB of HBM per device.

```python
import jax
import jax.numpy as jnp
from jax import lax

LEV = 4
CLAT = 32
NLAT = 512
NLON = 4096
N_LAT = 16


def with_ends(result, key, smallest, top_value):
    shape = result.shape
    place = [jax.random.randint(jax.random.fold_in(key, axis), (), 0, shape[axis]) for axis in range(len(shape))]
    result = result.at[tuple(place)].set(smallest)
    longest = shape.index(max(shape))
    place[longest] = (place[longest] + 1) % shape[longest]
    return result.at[tuple(place)].set(top_value)


def shard_levels(own_key, shape, shards, least, high):
    level = 1.0
    for position, shards_of in shards:
        heights = jax.random.uniform(jax.random.fold_in(jax.random.fold_in(own_key, 6), position), (shards_of,), jnp.float32, least / len(shards), high / len(shards))
        level = level * jnp.repeat(jnp.exp(heights), shape[position] // shards_of).reshape((-1,) + (1,) * (len(shape) - 1 - position))
    return level


def noise(stream_key, shape, spread, limit, pieces=(), held_as=jnp.bfloat16):
    gain = shard_levels(stream_key, shape, pieces, -0.22, 0.18) if pieces else 1.0
    result = jax.random.normal(stream_key, shape, jnp.float32) * spread * gain
    return jnp.minimum(jnp.maximum(result, -limit), limit).astype(held_as)


def setup_inputs(seed: int = 0) -> dict:
    key_of = jax.random.split(jax.random.key(seed), 5)
    state = noise(key_of[0], (4, LEV, NLAT, NLON), 0.5, 3.0, ((2, 16), (3, 16)), jnp.float32)
    cotangent = noise(key_of[1], (4, LEV, NLAT, NLON), 1.0, 6.0, ((2, 16), (3, 16)), jnp.float32)
    seamask = with_ends((jax.random.randint(key_of[2], (NLAT, NLON), 0, 5) < 4).astype(jnp.int32), jax.random.fold_in(key_of[2], 1), 0, 1)
    levels = with_ends(jax.random.randint(key_of[3], (NLAT, NLON), 1, LEV + 1), jax.random.fold_in(key_of[3], 1), 1, LEV).astype(jnp.int32)
    return {"state": state, "cotangent": cotangent, "seamask": seamask, "levels": levels}


courant = 0.4
vert_mix = 0.1
rotation = 0.3
buoyancy = 0.3
bottom_drag = 0.2

def slab_of(values, start, length, along):
    return lax.slice_in_dim(values, start, start + length, axis=values.ndim + along)

def face_div(fields, speeds, wet_mask, along):
    extent = fields.shape[along]
    faces = extent - 5
    cells = [slab_of(fields, offset, faces, along) for offset in range(6)]
    face_speed = 0.5 * (slab_of(speeds, 2, faces, along) + slab_of(speeds, 3, faces, along))
    open_face = slab_of(wet_mask, 2, faces, along) * slab_of(wet_mask, 3, faces, along)
    central = (37.0 * (cells[2] + cells[3]) - 8.0 * (cells[1] + cells[4]) + (cells[0] + cells[5])) / 60.0
    damping = (10.0 * (cells[3] - cells[2]) - 5.0 * (cells[4] - cells[1]) + (cells[5] - cells[0])) / 60.0
    flux = open_face * (face_speed * central - jnp.sqrt(face_speed * face_speed + 0.0001) * damping)
    return slab_of(flux, 1, faces - 1, along) - slab_of(flux, 0, faces - 1, along)

def advance(padded, sea_rim, level_rim, first_row, lat_total):
    level_count = padded.shape[1]
    lat_cells = padded.shape[2]
    lon_cells = padded.shape[3]
    level_index = jnp.arange(level_count, dtype=jnp.int32)[:, None, None]
    wet_mask = (sea_rim[None] * (level_index < level_rim[None]).astype(jnp.int32)).astype(jnp.float32)
    bottom = (sea_rim[None] * (level_index == level_rim[None] - 1).astype(jnp.int32)).astype(jnp.float32)
    divergence = face_div(padded, padded[2], wet_mask, -1)[:, :, 3:lat_cells - 3, :]
    divergence = divergence + face_div(padded, padded[3], wet_mask, -2)[:, :, :, 3:lon_cells - 3]
    center = padded[:, :, 3:lat_cells - 3, 3:lon_cells - 3]
    wet_center = wet_mask[:, 3:lat_cells - 3, 3:lon_cells - 3]
    bottom_center = bottom[:, 3:lat_cells - 3, 3:lon_cells - 3]
    zero_level = jnp.zeros_like(center[:, :1])
    zero_wet = jnp.zeros_like(wet_center[:1])
    above_cells = jnp.concatenate([zero_level, center[:, :-1]], axis=1)
    below_cells = jnp.concatenate([center[:, 1:], zero_level], axis=1)
    wet_above = jnp.concatenate([zero_wet, wet_center[:-1]], axis=0)
    wet_below = jnp.concatenate([wet_center[1:], zero_wet], axis=0)
    vertical = vert_mix * (wet_above * (above_cells - center) + wet_below * (below_cells - center))
    density = (-0.2 * padded[0] + 0.8 * padded[1]) * wet_mask
    pressure = buoyancy * jnp.cumsum(density, axis=0)
    press_east = 0.5 * (pressure[:, 3:lat_cells - 3, 4:lon_cells - 2] - pressure[:, 3:lat_cells - 3, 2:lon_cells - 4])
    press_north = 0.5 * (pressure[:, 4:lat_cells - 2, 3:lon_cells - 3] - pressure[:, 2:lat_cells - 4, 3:lon_cells - 3])
    row_index = (first_row + 3 + jnp.arange(lat_cells - 6, dtype=jnp.int32)).astype(jnp.float32)
    latitude = jnp.pi * ((row_index + 0.5) / lat_total - 0.5)
    coriolis = (rotation * jnp.sin(latitude))[:, None]
    east_now = center[2]
    north_now = center[3]
    force_east = coriolis * north_now - press_east - bottom_drag * bottom_center * east_now
    force_north = -coriolis * east_now - press_north - bottom_drag * bottom_center * north_now
    forcing = jnp.concatenate([jnp.zeros_like(center[:2]), jnp.stack([force_east, force_north])], axis=0)
    return (center - courant * divergence + vertical + forcing) * wet_center[None]

def wrap_lon(values, rim_width):
    return jnp.concatenate([values[..., -rim_width:], values, values[..., :rim_width]], axis=-1)

def reference(state, cotangent, seamask, levels):
    margin = 12
    lat_padded = jnp.pad(state, ((0, 0), (0, 0), (margin, margin), (0, 0)))
    cot_padded = jnp.pad(cotangent, ((0, 0), (0, 0), (6, 6), (0, 0)))
    sea_padded = jnp.pad(seamask, ((margin, margin), (0, 0)))
    lev_padded = jnp.pad(levels, ((margin, margin), (0, 0)))

    def one_block(block):
        start = (block * CLAT).astype(jnp.int32)
        slab = lax.dynamic_slice_in_dim(lat_padded, start, CLAT + 2 * margin, axis=2)
        sea_slab = wrap_lon(lax.dynamic_slice_in_dim(sea_padded, start, CLAT + 2 * margin, axis=0), 6)
        lev_slab = wrap_lon(lax.dynamic_slice_in_dim(lev_padded, start, CLAT + 2 * margin, axis=0), 6)
        cot_slab = lax.dynamic_slice_in_dim(cot_padded, start, CLAT + 12, axis=2)
        first_row = start - margin

        def two_steps(rows_in):
            half_way = advance(wrap_lon(rows_in, 6), sea_slab, lev_slab, first_row, NLAT)
            return advance(half_way, sea_slab[3:-3, 3:-3], lev_slab[3:-3, 3:-3], first_row + 3, NLAT)
        ahead, backward = jax.vjp(two_steps, slab)
        gradient = backward(cot_slab)[0]
        return (ahead[:, :, 6:6 + CLAT], gradient[:, :, margin:margin + CLAT])
    finals, grads = lax.map(one_block, jnp.arange(N_LAT, dtype=jnp.int32))
    final_state = jnp.moveaxis(finals, 0, 2).reshape(4, LEV, NLAT, NLON)
    adjoint_state = jnp.moveaxis(grads, 0, 2).reshape(4, LEV, NLAT, NLON)
    return (final_state, adjoint_state)
```

```python
import jax
import jax.numpy as jnp
from jax import lax
from jax.sharding import PartitionSpec as P

courant = 0.4
vert_mix = 0.1
rotation = 0.3
buoyancy = 0.3
bottom_drag = 0.2


def slab_of(values, start, length, along):
    return lax.slice_in_dim(values, start, start + length, axis=values.ndim + along)


def face_div(fields, speeds, wet_mask, along):
    extent = fields.shape[along]
    faces = extent - 5
    cells = [slab_of(fields, offset, faces, along) for offset in range(6)]
    face_speed = 0.5 * (slab_of(speeds, 2, faces, along) + slab_of(speeds, 3, faces, along))
    open_face = slab_of(wet_mask, 2, faces, along) * slab_of(wet_mask, 3, faces, along)
    central = (
        37.0 * (cells[2] + cells[3]) - 8.0 * (cells[1] + cells[4]) + (cells[0] + cells[5])
    ) / 60.0
    damping = (
        10.0 * (cells[3] - cells[2]) - 5.0 * (cells[4] - cells[1]) + (cells[5] - cells[0])
    ) / 60.0
    flux = open_face * (face_speed * central - jnp.sqrt(face_speed * face_speed + 0.0001) * damping)
    return slab_of(flux, 1, faces - 1, along) - slab_of(flux, 0, faces - 1, along)


def advance(padded, sea_rim, level_rim, first_row, lat_total):
    level_count = padded.shape[1]
    lat_cells = padded.shape[2]
    lon_cells = padded.shape[3]
    level_index = jnp.arange(level_count, dtype=jnp.int32)[:, None, None]
    wet_mask = (sea_rim[None] * (level_index < level_rim[None]).astype(jnp.int32)).astype(
        jnp.float32
    )
    bottom = (sea_rim[None] * (level_index == level_rim[None] - 1).astype(jnp.int32)).astype(
        jnp.float32
    )
    divergence = face_div(padded, padded[2], wet_mask, -1)[:, :, 3 : lat_cells - 3, :]
    divergence = divergence + face_div(padded, padded[3], wet_mask, -2)[:, :, :, 3 : lon_cells - 3]
    center = padded[:, :, 3 : lat_cells - 3, 3 : lon_cells - 3]
    wet_center = wet_mask[:, 3 : lat_cells - 3, 3 : lon_cells - 3]
    bottom_center = bottom[:, 3 : lat_cells - 3, 3 : lon_cells - 3]
    zero_level = jnp.zeros_like(center[:, :1])
    zero_wet = jnp.zeros_like(wet_center[:1])
    above_cells = jnp.concatenate([zero_level, center[:, :-1]], axis=1)
    below_cells = jnp.concatenate([center[:, 1:], zero_level], axis=1)
    wet_above = jnp.concatenate([zero_wet, wet_center[:-1]], axis=0)
    wet_below = jnp.concatenate([wet_center[1:], zero_wet], axis=0)
    vertical = vert_mix * (wet_above * (above_cells - center) + wet_below * (below_cells - center))
    density = (-0.2 * padded[0] + 0.8 * padded[1]) * wet_mask
    pressure = buoyancy * jnp.cumsum(density, axis=0)
    press_east = 0.5 * (
        pressure[:, 3 : lat_cells - 3, 4 : lon_cells - 2]
        - pressure[:, 3 : lat_cells - 3, 2 : lon_cells - 4]
    )
    press_north = 0.5 * (
        pressure[:, 4 : lat_cells - 2, 3 : lon_cells - 3]
        - pressure[:, 2 : lat_cells - 4, 3 : lon_cells - 3]
    )
    row_index = (first_row + 3 + jnp.arange(lat_cells - 6, dtype=jnp.int32)).astype(jnp.float32)
    latitude = jnp.pi * ((row_index + 0.5) / lat_total - 0.5)
    coriolis = (rotation * jnp.sin(latitude))[:, None]
    east_now = center[2]
    north_now = center[3]
    force_east = coriolis * north_now - press_east - bottom_drag * bottom_center * east_now
    force_north = -coriolis * east_now - press_north - bottom_drag * bottom_center * north_now
    forcing = jnp.concatenate(
        [jnp.zeros_like(center[:2]), jnp.stack([force_east, force_north])], axis=0
    )
    return (center - courant * divergence + vertical + forcing) * wet_center[None]


def halo(block, sides, width):
    for axis, dim in sides:
        count = lax.axis_size(axis)
        forward = [(i, (i + 1) % count) for i in range(count)]
        backward = [(target, source) for source, target in forward]
        low = lax.ppermute(
            lax.slice_in_dim(block, block.shape[dim] - width, None, axis=dim), axis, forward
        )
        high = lax.ppermute(lax.slice_in_dim(block, 0, width, axis=dim), axis, backward)
        block = jnp.concatenate([low, block, high], axis=dim)
    return block


def inside_rows(lat_start, rim_depth, row_count, lat_total):
    global_row = lat_start - rim_depth + jnp.arange(row_count + 2 * rim_depth, dtype=jnp.int32)
    return ((global_row >= 0) & (global_row < lat_total))[:, None]


def shards(state, cotangent, seamask, levels):
    fields, level_count, row_count, col_count = state.shape
    lat_total = row_count * lax.axis_size("lat")
    lat_start = lax.axis_index("lat") * row_count
    margin = 12
    reach = 6
    planes = jnp.concatenate(
        [
            state.reshape(fields * level_count, row_count, col_count),
            seamask.astype(jnp.float32)[None],
            levels.astype(jnp.float32)[None],
        ],
        axis=0,
    )
    wide = halo(planes, (("lon", 2), ("lat", 1)), margin)
    cot_wide = halo(
        cotangent.reshape(fields * level_count, row_count, col_count), (("lon", 2), ("lat", 1)), reach
    )
    inside = inside_rows(lat_start, margin, row_count, lat_total)
    cot_inside = inside_rows(lat_start, reach, row_count, lat_total)
    wide = wide * inside.astype(jnp.float32)
    cot_wide = cot_wide * cot_inside.astype(jnp.float32)
    slab = wide[: fields * level_count].reshape(fields, level_count, *wide.shape[1:])
    cot_slab = cot_wide.reshape(fields, level_count, *cot_wide.shape[1:])
    sea_slab = wide[fields * level_count].astype(jnp.int32)
    lev_slab = wide[fields * level_count + 1].astype(jnp.int32)
    first_row = lat_start - margin

    def two_steps(rows_in):
        half_way = advance(rows_in, sea_slab, lev_slab, first_row, lat_total)
        return advance(half_way, sea_slab[3:-3, 3:-3], lev_slab[3:-3, 3:-3], first_row + 3, lat_total)

    ahead, backward = jax.vjp(two_steps, slab)
    gradient = backward(cot_slab)[0]
    final_state = ahead[:, :, reach : reach + row_count, reach : reach + col_count]
    adjoint_state = gradient[:, :, margin : margin + row_count, margin : margin + col_count]
    return (final_state, adjoint_state)


def solution(mesh):
    placed = (
        P(None, None, "lat", "lon"),
        P(None, None, "lat", "lon"),
        P("lat", "lon"),
        P("lat", "lon"),
    )
    return jax.shard_map(
        shards,
        mesh=mesh,
        in_specs=placed,
        out_specs=(P(None, None, "lat", "lon"), P(None, None, "lat", "lon")),
        check_vma=False,
    )
```

```python
import jax
import jax.numpy as jnp
from jax import lax
from jax.sharding import PartitionSpec as P

courant = 0.4
vert_mix = 0.1
rotation = 0.3
buoyancy = 0.3
bottom_drag = 0.2


def slab_of(values, start, length, along):
    return lax.slice_in_dim(values, start, start + length, axis=values.ndim + along)


def face_div(fields, speeds, wet_mask, along):
    extent = fields.shape[along]
    faces = extent - 5
    cells = [slab_of(fields, offset, faces, along) for offset in range(6)]
    face_speed = 0.5 * (slab_of(speeds, 2, faces, along) + slab_of(speeds, 3, faces, along))
    open_face = slab_of(wet_mask, 2, faces, along) * slab_of(wet_mask, 3, faces, along)
    central = (
        37.0 * (cells[2] + cells[3]) - 8.0 * (cells[1] + cells[4]) + (cells[0] + cells[5])
    ) / 60.0
    damping = (
        10.0 * (cells[3] - cells[2]) - 5.0 * (cells[4] - cells[1]) + (cells[5] - cells[0])
    ) / 60.0
    flux = open_face * (face_speed * central - jnp.sqrt(face_speed * face_speed + 0.0001) * damping)
    return slab_of(flux, 1, faces - 1, along) - slab_of(flux, 0, faces - 1, along)


def advance(padded, sea_rim, level_rim, first_row, lat_total):
    level_count = padded.shape[1]
    lat_cells = padded.shape[2]
    lon_cells = padded.shape[3]
    level_index = jnp.arange(level_count, dtype=jnp.int32)[:, None, None]
    wet_mask = (sea_rim[None] * (level_index < level_rim[None]).astype(jnp.int32)).astype(
        jnp.float32
    )
    bottom = (sea_rim[None] * (level_index == level_rim[None] - 1).astype(jnp.int32)).astype(
        jnp.float32
    )
    divergence = face_div(padded, padded[2], wet_mask, -1)[:, :, 3 : lat_cells - 3, :]
    divergence = divergence + face_div(padded, padded[3], wet_mask, -2)[:, :, :, 3 : lon_cells - 3]
    center = padded[:, :, 3 : lat_cells - 3, 3 : lon_cells - 3]
    wet_center = wet_mask[:, 3 : lat_cells - 3, 3 : lon_cells - 3]
    bottom_center = bottom[:, 3 : lat_cells - 3, 3 : lon_cells - 3]
    zero_level = jnp.zeros_like(center[:, :1])
    zero_wet = jnp.zeros_like(wet_center[:1])
    above_cells = jnp.concatenate([zero_level, center[:, :-1]], axis=1)
    below_cells = jnp.concatenate([center[:, 1:], zero_level], axis=1)
    wet_above = jnp.concatenate([zero_wet, wet_center[:-1]], axis=0)
    wet_below = jnp.concatenate([wet_center[1:], zero_wet], axis=0)
    vertical = vert_mix * (wet_above * (above_cells - center) + wet_below * (below_cells - center))
    density = (-0.2 * padded[0] + 0.8 * padded[1]) * wet_mask
    pressure = buoyancy * jnp.cumsum(density, axis=0)
    press_east = 0.5 * (
        pressure[:, 3 : lat_cells - 3, 4 : lon_cells - 2]
        - pressure[:, 3 : lat_cells - 3, 2 : lon_cells - 4]
    )
    press_north = 0.5 * (
        pressure[:, 4 : lat_cells - 2, 3 : lon_cells - 3]
        - pressure[:, 2 : lat_cells - 4, 3 : lon_cells - 3]
    )
    row_index = (first_row + 3 + jnp.arange(lat_cells - 6, dtype=jnp.int32)).astype(jnp.float32)
    latitude = jnp.pi * ((row_index + 0.5) / lat_total - 0.5)
    coriolis = (rotation * jnp.sin(latitude))[:, None]
    east_now = center[2]
    north_now = center[3]
    force_east = coriolis * north_now - press_east - bottom_drag * bottom_center * east_now
    force_north = -coriolis * east_now - press_north - bottom_drag * bottom_center * north_now
    forcing = jnp.concatenate(
        [jnp.zeros_like(center[:2]), jnp.stack([force_east, force_north])], axis=0
    )
    return (center - courant * divergence + vertical + forcing) * wet_center[None]


def halo(block, sides, width):
    for axis, dim in sides:
        count = lax.axis_size(axis)
        forward = [(i, (i + 1) % count) for i in range(count)]
        backward = [(target, source) for source, target in forward]
        low = lax.ppermute(
            lax.slice_in_dim(block, block.shape[dim] - width, None, axis=dim), axis, forward
        )
        high = lax.ppermute(lax.slice_in_dim(block, 0, width, axis=dim), axis, backward)
        block = jnp.concatenate([low, block, high], axis=dim)
    return block


def inside_rows(lat_start, rim_depth, row_count, lat_total):
    global_row = lat_start - rim_depth + jnp.arange(row_count + 2 * rim_depth, dtype=jnp.int32)
    return ((global_row >= 0) & (global_row < lat_total))[:, None]


def shards(state, cotangent, seamask, levels):
    fields, level_count, row_count, col_count = state.shape
    lat_total = row_count * lax.axis_size("lat")
    lat_start = lax.axis_index("lat") * row_count
    margin = 12
    reach = 6
    planes = fields * level_count
    stacked = jnp.concatenate(
        [
            state.reshape(planes, row_count, col_count),
            cotangent.reshape(planes, row_count, col_count),
            seamask.astype(jnp.float32)[None],
            levels.astype(jnp.float32)[None],
        ],
        axis=0,
    )
    wide = halo(stacked, (("lon", 2), ("lat", 1)), margin)
    inside = inside_rows(lat_start, margin, row_count, lat_total)
    wide = wide * inside.astype(jnp.float32)
    cut = margin - reach
    slab = wide[:planes].reshape(fields, level_count, *wide.shape[1:])
    cot_slab = wide[planes : 2 * planes, cut:-cut, cut:-cut].reshape(
        fields, level_count, row_count + 2 * reach, col_count + 2 * reach
    )
    sea_slab = wide[2 * planes].astype(jnp.int32)
    lev_slab = wide[2 * planes + 1].astype(jnp.int32)
    first_row = lat_start - margin

    def two_steps(rows_in):
        half_way = advance(rows_in, sea_slab, lev_slab, first_row, lat_total)
        return advance(half_way, sea_slab[3:-3, 3:-3], lev_slab[3:-3, 3:-3], first_row + 3, lat_total)

    ahead, backward = jax.vjp(two_steps, slab)
    gradient = backward(cot_slab)[0]
    final_state = ahead[:, :, reach : reach + row_count, reach : reach + col_count]
    adjoint_state = gradient[:, :, margin : margin + row_count, margin : margin + col_count]
    return (final_state, adjoint_state)


def solution(mesh):
    placed = (
        P(None, None, "lat", "lon"),
        P(None, None, "lat", "lon"),
        P("lat", "lon"),
        P("lat", "lon"),
    )
    return jax.shard_map(
        shards,
        mesh=mesh,
        in_specs=placed,
        out_specs=(P(None, None, "lat", "lon"), P(None, None, "lat", "lon")),
        check_vma=False,
    )
```

```python
import jax
import jax.numpy as jnp
from jax import lax
from jax.sharding import PartitionSpec as P

courant = 0.4
vert_mix = 0.1
rotation = 0.3
buoyancy = 0.3
bottom_drag = 0.2


def slab_of(values, start, length, along):
    return lax.slice_in_dim(values, start, start + length, axis=values.ndim + along)


def face_div(fields, speeds, wet_mask, along):
    extent = fields.shape[along]
    faces = extent - 5
    cells = [slab_of(fields, offset, faces, along) for offset in range(6)]
    face_speed = 0.5 * (slab_of(speeds, 2, faces, along) + slab_of(speeds, 3, faces, along))
    open_face = slab_of(wet_mask, 2, faces, along) * slab_of(wet_mask, 3, faces, along)
    central = (
        37.0 * (cells[2] + cells[3]) - 8.0 * (cells[1] + cells[4]) + (cells[0] + cells[5])
    ) / 60.0
    damping = (
        10.0 * (cells[3] - cells[2]) - 5.0 * (cells[4] - cells[1]) + (cells[5] - cells[0])
    ) / 60.0
    flux = open_face * (face_speed * central - jnp.sqrt(face_speed * face_speed + 0.0001) * damping)
    return slab_of(flux, 1, faces - 1, along) - slab_of(flux, 0, faces - 1, along)


def advance(padded, sea_rim, level_rim, first_row, lat_total):
    level_count = padded.shape[1]
    lat_cells = padded.shape[2]
    lon_cells = padded.shape[3]
    level_index = jnp.arange(level_count, dtype=jnp.int32)[:, None, None]
    wet_mask = (sea_rim[None] * (level_index < level_rim[None]).astype(jnp.int32)).astype(
        jnp.float32
    )
    bottom = (sea_rim[None] * (level_index == level_rim[None] - 1).astype(jnp.int32)).astype(
        jnp.float32
    )
    divergence = face_div(padded, padded[2], wet_mask, -1)[:, :, 3 : lat_cells - 3, :]
    divergence = divergence + face_div(padded, padded[3], wet_mask, -2)[:, :, :, 3 : lon_cells - 3]
    center = padded[:, :, 3 : lat_cells - 3, 3 : lon_cells - 3]
    wet_center = wet_mask[:, 3 : lat_cells - 3, 3 : lon_cells - 3]
    bottom_center = bottom[:, 3 : lat_cells - 3, 3 : lon_cells - 3]
    zero_level = jnp.zeros_like(center[:, :1])
    zero_wet = jnp.zeros_like(wet_center[:1])
    above_cells = jnp.concatenate([zero_level, center[:, :-1]], axis=1)
    below_cells = jnp.concatenate([center[:, 1:], zero_level], axis=1)
    wet_above = jnp.concatenate([zero_wet, wet_center[:-1]], axis=0)
    wet_below = jnp.concatenate([wet_center[1:], zero_wet], axis=0)
    vertical = vert_mix * (wet_above * (above_cells - center) + wet_below * (below_cells - center))
    density = (-0.2 * padded[0] + 0.8 * padded[1]) * wet_mask
    pressure = buoyancy * jnp.cumsum(density, axis=0)
    press_east = 0.5 * (
        pressure[:, 3 : lat_cells - 3, 4 : lon_cells - 2]
        - pressure[:, 3 : lat_cells - 3, 2 : lon_cells - 4]
    )
    press_north = 0.5 * (
        pressure[:, 4 : lat_cells - 2, 3 : lon_cells - 3]
        - pressure[:, 2 : lat_cells - 4, 3 : lon_cells - 3]
    )
    row_index = (first_row + 3 + jnp.arange(lat_cells - 6, dtype=jnp.int32)).astype(jnp.float32)
    latitude = jnp.pi * ((row_index + 0.5) / lat_total - 0.5)
    coriolis = (rotation * jnp.sin(latitude))[:, None]
    east_now = center[2]
    north_now = center[3]
    force_east = coriolis * north_now - press_east - bottom_drag * bottom_center * east_now
    force_north = -coriolis * east_now - press_north - bottom_drag * bottom_center * north_now
    forcing = jnp.concatenate(
        [jnp.zeros_like(center[:2]), jnp.stack([force_east, force_north])], axis=0
    )
    return (center - courant * divergence + vertical + forcing) * wet_center[None]


def ring(count, step):
    return [(i, (i + step) % count) for i in range(count)]


def send_packed(pieces, axis, pairs):
    flat = jnp.concatenate([piece.reshape(-1) for piece in pieces])
    size = flat.shape[0]
    rows = -(-size // 1024) * 8
    flat = jnp.pad(flat, (0, rows * 128 - size)).reshape(rows, 128)
    flat = lax.ppermute(flat, axis, pairs).reshape(-1)
    out = []
    offset = 0
    for piece in pieces:
        out.append(flat[offset : offset + piece.size].reshape(piece.shape))
        offset += piece.size
    return out


def extend_pair(blocks, widths, axis, dim):
    count = lax.axis_size(axis)
    lows = send_packed(
        [lax.slice_in_dim(b, b.shape[dim] - w, None, axis=dim) for b, w in zip(blocks, widths)],
        axis,
        ring(count, 1),
    )
    highs = send_packed(
        [lax.slice_in_dim(b, 0, w, axis=dim) for b, w in zip(blocks, widths)], axis, ring(count, -1)
    )
    return [jnp.concatenate([lo, b, hi], axis=dim) for lo, b, hi in zip(lows, blocks, highs)]


def inside_rows(lat_start, rim_depth, row_count, lat_total):
    global_row = lat_start - rim_depth + jnp.arange(row_count + 2 * rim_depth, dtype=jnp.int32)
    return ((global_row >= 0) & (global_row < lat_total))[:, None]


def shards(state, cotangent, seamask, levels):
    fields, level_count, row_count, col_count = state.shape
    lat_total = row_count * lax.axis_size("lat")
    lat_start = lax.axis_index("lat") * row_count
    margin = 12
    reach = 6
    depth = (seamask * levels).astype(jnp.float32)
    blocks = [state, cotangent, depth]
    widths = [margin, reach, margin]
    blocks = extend_pair(blocks, widths, "lon", -1)
    blocks = extend_pair(blocks, widths, "lat", -2)
    slab, cot_slab, depth_slab = blocks
    slab = slab * inside_rows(lat_start, margin, row_count, lat_total).astype(jnp.float32)
    cot_slab = cot_slab * inside_rows(lat_start, reach, row_count, lat_total).astype(jnp.float32)
    depth_slab = depth_slab * inside_rows(lat_start, margin, row_count, lat_total).astype(jnp.float32)
    sea_slab = (depth_slab > 0.5).astype(jnp.int32)
    lev_slab = depth_slab.astype(jnp.int32)
    first_row = lat_start - margin

    def two_steps(rows_in):
        half_way = advance(rows_in, sea_slab, lev_slab, first_row, lat_total)
        return advance(half_way, sea_slab[3:-3, 3:-3], lev_slab[3:-3, 3:-3], first_row + 3, lat_total)

    ahead, backward = jax.vjp(two_steps, slab)
    gradient = backward(cot_slab)[0]
    final_state = ahead[:, :, reach : reach + row_count, reach : reach + col_count]
    adjoint_state = gradient[:, :, margin : margin + row_count, margin : margin + col_count]
    return (final_state, adjoint_state)


def solution(mesh):
    placed = (
        P(None, None, "lat", "lon"),
        P(None, None, "lat", "lon"),
        P("lat", "lon"),
        P("lat", "lon"),
    )
    return jax.shard_map(
        shards,
        mesh=mesh,
        in_specs=placed,
        out_specs=(P(None, None, "lat", "lon"), P(None, None, "lat", "lon")),
        check_vma=False,
    )
```

```python
import jax
import jax.numpy as jnp
from jax import lax
from jax.sharding import PartitionSpec as P
from jax.experimental import pallas as pl
from jax.experimental.pallas import tpu as pltpu
import functools

courant = 0.4
vert_mix = 0.1
rotation = 0.3
buoyancy = 0.3
bottom_drag = 0.2


SIXTIETH = 1.0 / 60.0
INTERPRET = False
CENTRAL = {-2: 1.0, -1: -8.0, 0: 37.0, 1: 37.0, 2: -8.0, 3: 1.0}
DAMPING = {-2: -1.0, -1: 5.0, 0: -10.0, 1: 10.0, 2: -5.0, 3: 1.0}


def shifted(x, step, axis):
    n = x.shape[axis]
    step = step % n
    if step == 0:
        return x
    return pltpu.roll(x, n - step, axis)


def wet_of(depth, k):
    return jnp.where(depth > k + 0.5, 1.0, 0.0)


def bottom_of(depth, k):
    return jnp.where(jnp.abs(depth - (k + 1.0)) < 0.5, 1.0, 0.0)


def face_terms(q, axis):
    m2 = shifted(q, -2, axis)
    m1 = shifted(q, -1, axis)
    p1 = shifted(q, 1, axis)
    p2 = shifted(q, 2, axis)
    p3 = shifted(q, 3, axis)
    central = (37.0 * (q + p1) - 8.0 * (m1 + p2) + (m2 + p3)) * SIXTIETH
    damping = (10.0 * (p1 - q) - 5.0 * (p2 - m1) + (p3 - m2)) * SIXTIETH
    return central, damping


def face_speed(wet, speed, axis):
    open_face = wet * shifted(wet, 1, axis)
    w = 0.5 * (speed + shifted(speed, 1, axis))
    s = jnp.sqrt(w * w + 0.0001)
    return open_face, w, s


def forward(src, store, depth, cor):
    level_count = src.shape[1]
    column = None
    for k in range(level_count):
        wet = wet_of(depth, k)
        bottom = bottom_of(depth, k)
        q = [src[f, k] for f in range(4)]
        density = (-0.2 * q[0] + 0.8 * q[1]) * wet
        column = density if column is None else column + density
        pressure = buoyancy * column
        div = [None] * 4
        for axis, speed in ((1, q[2]), (0, q[3])):
            open_face, w, s = face_speed(wet, speed, axis)
            for f in range(4):
                central, damping = face_terms(q[f], axis)
                flux = open_face * (w * central - s * damping)
                part = flux - shifted(flux, -1, axis)
                div[f] = part if div[f] is None else div[f] + part
        press_east = 0.5 * (shifted(pressure, 1, 1) - shifted(pressure, -1, 1))
        press_north = 0.5 * (shifted(pressure, 1, 0) - shifted(pressure, -1, 0))
        force = [
            None,
            None,
            cor * q[3] - press_east - bottom_drag * bottom * q[2],
            -cor * q[2] - press_north - bottom_drag * bottom * q[3],
        ]
        for f in range(4):
            vertical = None
            if k > 0:
                vertical = wet_of(depth, k - 1) * (src[f, k - 1] - q[f])
            if k < level_count - 1:
                below = wet_of(depth, k + 1) * (src[f, k + 1] - q[f])
                vertical = below if vertical is None else vertical + below
            value = q[f] - courant * div[f] + vert_mix * vertical
            if force[f] is not None:
                value = value + force[f]
            store(f, k, value * wet)


def backward(x, lam, store, g_ref, depth, cor):
    level_count = x.shape[1]
    for k in range(level_count):
        wet = wet_of(depth, k)
        for f in range(4):
            g_ref[f, k] = wet * lam[f, k]
    density_bar = [None] * level_count
    column = None
    for k in reversed(range(level_count)):
        gu = g_ref[2, k]
        gv = g_ref[3, k]
        pbar = 0.5 * (shifted(gu, 1, 1) - shifted(gu, -1, 1)) + 0.5 * (
            shifted(gv, 1, 0) - shifted(gv, -1, 0)
        )
        column = pbar if column is None else column + pbar
        density_bar[k] = buoyancy * column
    for k in range(level_count):
        wet = wet_of(depth, k)
        bottom = bottom_of(depth, k)
        q = [x[f, k] for f in range(4)]
        g = [g_ref[f, k] for f in range(4)]
        acc = list(g)
        for f in range(4):
            vertical = None
            if k > 0:
                vertical = wet * g_ref[f, k - 1] - wet_of(depth, k - 1) * g[f]
            if k < level_count - 1:
                below = wet * g_ref[f, k + 1] - wet_of(depth, k + 1) * g[f]
                vertical = below if vertical is None else vertical + below
            acc[f] = acc[f] + vert_mix * vertical
        acc[2] = acc[2] - bottom_drag * bottom * g[2] - cor * g[3]
        acc[3] = acc[3] + cor * g[2] - bottom_drag * bottom * g[3]
        acc[0] = acc[0] - 0.2 * wet * density_bar[k]
        acc[1] = acc[1] + 0.8 * wet * density_bar[k]
        div_bar = [-courant * g[f] for f in range(4)]
        for axis, speed_field in ((1, 2), (0, 3)):
            open_face, w, s = face_speed(wet, q[speed_field], axis)
            ratio = w / s
            w_bar = None
            for f in range(4):
                flux_bar = open_face * (div_bar[f] - shifted(div_bar[f], 1, axis))
                central, damping = face_terms(q[f], axis)
                part = flux_bar * (central - ratio * damping)
                w_bar = part if w_bar is None else w_bar + part
                alpha = flux_bar * w * SIXTIETH
                beta = -flux_bar * s * SIXTIETH
                for j in range(-2, 4):
                    acc[f] = acc[f] + shifted(CENTRAL[j] * alpha + DAMPING[j] * beta, -j, axis)
            acc[speed_field] = acc[speed_field] + 0.5 * (w_bar + shifted(w_bar, -1, axis))
        for f in range(4):
            store(f, k, acc[f])


def two_step_kernel(margin, rows, cols, x0, lam, depth_ref, cor_ref, final_ref, grad_ref, x1, mu, g_ref):
    depth = depth_ref[...]
    cor = cor_ref[...]

    def crop(value):
        return shifted(shifted(value, margin, 0), margin, 1)[:rows, :cols]

    def keep(ref):
        def put(f, k, value):
            ref[f, k] = value
        return put

    def keep_cropped(ref):
        def put(f, k, value):
            ref[f, k] = crop(value)
        return put

    forward(x0, keep(x1), depth, cor)
    forward(x1, keep_cropped(final_ref), depth, cor)
    backward(x1, lam, keep(mu), g_ref, depth, cor)
    backward(x0, mu, keep_cropped(grad_ref), g_ref, depth, cor)


def halo(block, sides, width):
    for axis, dim in sides:
        count = lax.axis_size(axis)
        forward_pairs = [(i, (i + 1) % count) for i in range(count)]
        backward_pairs = [(target, source) for source, target in forward_pairs]
        low = lax.ppermute(
            lax.slice_in_dim(block, block.shape[dim] - width, None, axis=dim), axis, forward_pairs
        )
        high = lax.ppermute(lax.slice_in_dim(block, 0, width, axis=dim), axis, backward_pairs)
        block = jnp.concatenate([low, block, high], axis=dim)
    return block


def inside_rows(lat_start, rim_depth, row_count, lat_total):
    global_row = lat_start - rim_depth + jnp.arange(row_count + 2 * rim_depth, dtype=jnp.int32)
    return ((global_row >= 0) & (global_row < lat_total))[:, None]


def shards(state, cotangent, seamask, levels):
    fields, level_count, row_count, col_count = state.shape
    lat_total = row_count * lax.axis_size("lat")
    lat_start = lax.axis_index("lat") * row_count
    margin = 12
    reach = 6
    planes = fields * level_count
    stacked = jnp.concatenate(
        [
            state.reshape(planes, row_count, col_count),
            (seamask * levels).astype(jnp.float32)[None],
        ],
        axis=0,
    )
    wide = halo(stacked, (("lon", 2), ("lat", 1)), margin)
    cot_wide = halo(
        cotangent.reshape(planes, row_count, col_count), (("lon", 2), ("lat", 1)), reach
    )
    wide = wide * inside_rows(lat_start, margin, row_count, lat_total).astype(jnp.float32)
    cot_wide = cot_wide * inside_rows(lat_start, reach, row_count, lat_total).astype(jnp.float32)
    frame_rows = row_count + 2 * margin
    frame_cols = -(-(col_count + 2 * margin) // 128) * 128
    extra = frame_cols - (col_count + 2 * margin)
    cut = margin - reach
    x0 = jnp.pad(wide[:planes], ((0, 0), (0, 0), (0, extra))).reshape(
        fields, level_count, frame_rows, frame_cols
    )
    depth = jnp.pad(wide[planes], ((0, 0), (0, extra)))
    lam = jnp.pad(cot_wide, ((0, 0), (cut, cut), (cut, cut + extra))).reshape(
        fields, level_count, frame_rows, frame_cols
    )
    row_index = (lat_start - margin + jnp.arange(frame_rows, dtype=jnp.int32)).astype(jnp.float32)
    latitude = jnp.pi * ((row_index + 0.5) / lat_total - 0.5)
    cor = jnp.broadcast_to((rotation * jnp.sin(latitude))[:, None], (frame_rows, frame_cols))
    frame = (fields, level_count, frame_rows, frame_cols)
    out_block = jax.ShapeDtypeStruct((fields, level_count, row_count, col_count), jnp.float32)
    vmem = pl.BlockSpec(memory_space=pltpu.VMEM)
    final_state, adjoint_state = pl.pallas_call(
        functools.partial(two_step_kernel, margin, row_count, col_count),
        out_shape=(out_block, out_block),
        in_specs=[vmem, vmem, vmem, vmem],
        out_specs=(vmem, vmem),
        scratch_shapes=[pltpu.VMEM(frame, jnp.float32) for _ in range(3)],
        interpret=INTERPRET,
    )(x0, lam, depth, cor)
    return (final_state, adjoint_state)


def solution(mesh):
    placed = (
        P(None, None, "lat", "lon"),
        P(None, None, "lat", "lon"),
        P("lat", "lon"),
        P("lat", "lon"),
    )
    return jax.shard_map(
        shards,
        mesh=mesh,
        in_specs=placed,
        out_specs=(P(None, None, "lat", "lon"), P(None, None, "lat", "lon")),
        check_vma=False,
    )
```

```python
import jax
import jax.numpy as jnp
from jax import lax
from jax.sharding import PartitionSpec as P
from jax.experimental import pallas as pl
from jax.experimental.pallas import tpu as pltpu
import functools

courant = 0.4
vert_mix = 0.1
rotation = 0.3
buoyancy = 0.3
bottom_drag = 0.2


SIXTIETH = 1.0 / 60.0
INTERPRET = False
CENTRAL = {-2: 1.0, -1: -8.0, 0: 37.0, 1: 37.0, 2: -8.0, 3: 1.0}
DAMPING = {-2: -1.0, -1: 5.0, 0: -10.0, 1: 10.0, 2: -5.0, 3: 1.0}


def shifted(x, step, axis):
    n = x.shape[axis]
    step = step % n
    if step == 0:
        return x
    return pltpu.roll(x, n - step, axis)


def wet_of(depth, k):
    return jnp.where(depth > k + 0.5, 1.0, 0.0)


def bottom_of(depth, k):
    return jnp.where(jnp.abs(depth - (k + 1.0)) < 0.5, 1.0, 0.0)


def face_terms(q, axis):
    m2 = shifted(q, -2, axis)
    m1 = shifted(q, -1, axis)
    p1 = shifted(q, 1, axis)
    p2 = shifted(q, 2, axis)
    p3 = shifted(q, 3, axis)
    central = (37.0 * (q + p1) - 8.0 * (m1 + p2) + (m2 + p3)) * SIXTIETH
    damping = (10.0 * (p1 - q) - 5.0 * (p2 - m1) + (p3 - m2)) * SIXTIETH
    return central, damping


def face_speed(wet, speed, axis):
    open_face = wet * shifted(wet, 1, axis)
    w = 0.5 * (speed + shifted(speed, 1, axis))
    s = jnp.sqrt(w * w + 0.0001)
    return open_face, w, s


def forward(src, store, depth, cor):
    level_count = src.shape[1]
    column = None
    for k in range(level_count):
        wet = wet_of(depth, k)
        bottom = bottom_of(depth, k)
        q = [src[f, k] for f in range(4)]
        density = (-0.2 * q[0] + 0.8 * q[1]) * wet
        column = density if column is None else column + density
        pressure = buoyancy * column
        div = [None] * 4
        for axis, speed in ((1, q[2]), (0, q[3])):
            open_face, w, s = face_speed(wet, speed, axis)
            for f in range(4):
                central, damping = face_terms(q[f], axis)
                flux = open_face * (w * central - s * damping)
                part = flux - shifted(flux, -1, axis)
                div[f] = part if div[f] is None else div[f] + part
        press_east = 0.5 * (shifted(pressure, 1, 1) - shifted(pressure, -1, 1))
        press_north = 0.5 * (shifted(pressure, 1, 0) - shifted(pressure, -1, 0))
        force = [
            None,
            None,
            cor * q[3] - press_east - bottom_drag * bottom * q[2],
            -cor * q[2] - press_north - bottom_drag * bottom * q[3],
        ]
        for f in range(4):
            vertical = None
            if k > 0:
                vertical = wet_of(depth, k - 1) * (src[f, k - 1] - q[f])
            if k < level_count - 1:
                below = wet_of(depth, k + 1) * (src[f, k + 1] - q[f])
                vertical = below if vertical is None else vertical + below
            value = q[f] - courant * div[f] + vert_mix * vertical
            if force[f] is not None:
                value = value + force[f]
            store(f, k, value * wet)


def backward(x, lam, store, g_ref, depth, cor):
    level_count = x.shape[1]
    for k in range(level_count):
        wet = wet_of(depth, k)
        for f in range(4):
            g_ref[f, k] = wet * lam[f, k]
    density_bar = [None] * level_count
    column = None
    for k in reversed(range(level_count)):
        gu = g_ref[2, k]
        gv = g_ref[3, k]
        pbar = 0.5 * (shifted(gu, 1, 1) - shifted(gu, -1, 1)) + 0.5 * (
            shifted(gv, 1, 0) - shifted(gv, -1, 0)
        )
        column = pbar if column is None else column + pbar
        density_bar[k] = buoyancy * column
    for k in range(level_count):
        wet = wet_of(depth, k)
        bottom = bottom_of(depth, k)
        q = [x[f, k] for f in range(4)]
        g = [g_ref[f, k] for f in range(4)]
        acc = list(g)
        for f in range(4):
            vertical = None
            if k > 0:
                vertical = wet * g_ref[f, k - 1] - wet_of(depth, k - 1) * g[f]
            if k < level_count - 1:
                below = wet * g_ref[f, k + 1] - wet_of(depth, k + 1) * g[f]
                vertical = below if vertical is None else vertical + below
            acc[f] = acc[f] + vert_mix * vertical
        acc[2] = acc[2] - bottom_drag * bottom * g[2] - cor * g[3]
        acc[3] = acc[3] + cor * g[2] - bottom_drag * bottom * g[3]
        acc[0] = acc[0] - 0.2 * wet * density_bar[k]
        acc[1] = acc[1] + 0.8 * wet * density_bar[k]
        div_bar = [-courant * g[f] for f in range(4)]
        for axis, speed_field in ((1, 2), (0, 3)):
            open_face, w, s = face_speed(wet, q[speed_field], axis)
            ratio = w / s
            w_bar = None
            for f in range(4):
                flux_bar = open_face * (div_bar[f] - shifted(div_bar[f], 1, axis))
                central, damping = face_terms(q[f], axis)
                part = flux_bar * (central - ratio * damping)
                w_bar = part if w_bar is None else w_bar + part
                alpha = flux_bar * w * SIXTIETH
                beta = -flux_bar * s * SIXTIETH
                for j in range(-2, 4):
                    acc[f] = acc[f] + shifted(CENTRAL[j] * alpha + DAMPING[j] * beta, -j, axis)
            acc[speed_field] = acc[speed_field] + 0.5 * (w_bar + shifted(w_bar, -1, axis))
        for f in range(4):
            store(f, k, acc[f])


def two_step_kernel(margin, rows, cols, x0, lam, depth_ref, cor_ref, final_ref, grad_ref, x1, mu, g_ref):
    depth = depth_ref[...]
    cor = cor_ref[...]

    def crop(value):
        return shifted(shifted(value, margin, 0), margin, 1)[:rows, :cols]

    def keep(ref):
        def put(f, k, value):
            ref[f, k] = value
        return put

    def keep_cropped(ref):
        def put(f, k, value):
            ref[f, k] = crop(value)
        return put

    forward(x0, keep(x1), depth, cor)
    forward(x1, keep_cropped(final_ref), depth, cor)
    backward(x1, lam, keep(mu), g_ref, depth, cor)
    backward(x0, mu, keep_cropped(grad_ref), g_ref, depth, cor)


def ring(count, step):
    return [(i, (i + step) % count) for i in range(count)]


def lat_round(blocks, widths):
    count = lax.axis_size("lat")
    cols = blocks[0].shape[-1]

    def message(take_last):
        parts = []
        for b, w in zip(blocks, widths):
            piece = b[:, b.shape[1] - w :, :] if take_last else b[:, :w, :]
            parts.append(piece.reshape(-1, cols))
        return jnp.concatenate(parts, axis=0)

    lows = lax.ppermute(message(True), "lat", ring(count, 1))
    highs = lax.ppermute(message(False), "lat", ring(count, -1))
    out = []
    offset = 0
    for b, w in zip(blocks, widths):
        n = b.shape[0] * w
        lo = lows[offset : offset + n].reshape(b.shape[0], w, cols)
        hi = highs[offset : offset + n].reshape(b.shape[0], w, cols)
        offset += n
        out.append(jnp.concatenate([lo, b, hi], axis=1))
    return out


def lon_round(blocks, width):
    count = lax.axis_size("lon")

    def message(take_last):
        parts = []
        for b in blocks:
            piece = b[:, :, b.shape[2] - width :] if take_last else b[:, :, :width]
            parts.append(jnp.transpose(piece, (2, 0, 1)).reshape(width, -1))
        return jnp.concatenate(parts, axis=1)

    lows = lax.ppermute(message(True), "lon", ring(count, 1))
    highs = lax.ppermute(message(False), "lon", ring(count, -1))
    out = []
    offset = 0
    for b in blocks:
        n = b.shape[0] * b.shape[1]
        lo = jnp.transpose(lows[:, offset : offset + n].reshape(width, b.shape[0], b.shape[1]), (1, 2, 0))
        hi = jnp.transpose(highs[:, offset : offset + n].reshape(width, b.shape[0], b.shape[1]), (1, 2, 0))
        offset += n
        out.append(jnp.concatenate([lo, b, hi], axis=2))
    return out


def inside_rows(lat_start, rim_depth, row_count, lat_total):
    global_row = lat_start - rim_depth + jnp.arange(row_count + 2 * rim_depth, dtype=jnp.int32)
    return ((global_row >= 0) & (global_row < lat_total))[:, None]


def shards(state, cotangent, seamask, levels):
    fields, level_count, row_count, col_count = state.shape
    lat_total = row_count * lax.axis_size("lat")
    lat_start = lax.axis_index("lat") * row_count
    margin = 12
    reach = 6
    planes = fields * level_count
    stacked = jnp.concatenate(
        [
            state.reshape(planes, row_count, col_count),
            (seamask * levels).astype(jnp.float32)[None],
        ],
        axis=0,
    )
    cot = cotangent.reshape(planes, row_count, col_count)
    wide, cot_wide = lat_round([stacked, cot], [margin, reach])
    wide, cot_wide = lon_round([wide, cot_wide], margin)
    wide = wide * inside_rows(lat_start, margin, row_count, lat_total).astype(jnp.float32)
    cot_wide = cot_wide * inside_rows(lat_start, reach, row_count, lat_total).astype(jnp.float32)
    frame_rows = row_count + 2 * margin
    frame_cols = -(-(col_count + 2 * margin) // 128) * 128
    extra = frame_cols - (col_count + 2 * margin)
    cut = margin - reach
    x0 = jnp.pad(wide[:planes], ((0, 0), (0, 0), (0, extra))).reshape(
        fields, level_count, frame_rows, frame_cols
    )
    depth = jnp.pad(wide[planes], ((0, 0), (0, extra)))
    lam = jnp.pad(cot_wide, ((0, 0), (cut, cut), (0, extra))).reshape(
        fields, level_count, frame_rows, frame_cols
    )
    row_index = (lat_start - margin + jnp.arange(frame_rows, dtype=jnp.int32)).astype(jnp.float32)
    latitude = jnp.pi * ((row_index + 0.5) / lat_total - 0.5)
    cor = jnp.broadcast_to((rotation * jnp.sin(latitude))[:, None], (frame_rows, frame_cols))
    frame = (fields, level_count, frame_rows, frame_cols)
    out_block = jax.ShapeDtypeStruct((fields, level_count, row_count, col_count), jnp.float32)
    vmem = pl.BlockSpec(memory_space=pltpu.VMEM)
    final_state, adjoint_state = pl.pallas_call(
        functools.partial(two_step_kernel, margin, row_count, col_count),
        out_shape=(out_block, out_block),
        in_specs=[vmem, vmem, vmem, vmem],
        out_specs=(vmem, vmem),
        scratch_shapes=[pltpu.VMEM(frame, jnp.float32) for _ in range(3)],
        interpret=INTERPRET,
    )(x0, lam, depth, cor)
    return (final_state, adjoint_state)


def solution(mesh):
    placed = (
        P(None, None, "lat", "lon"),
        P(None, None, "lat", "lon"),
        P("lat", "lon"),
        P("lat", "lon"),
    )
    return jax.shard_map(
        shards,
        mesh=mesh,
        in_specs=placed,
        out_specs=(P(None, None, "lat", "lon"), P(None, None, "lat", "lon")),
        check_vma=False,
    )
```

```python
import jax
import jax.numpy as jnp
from jax import lax
from jax.sharding import PartitionSpec as P
from jax.experimental import pallas as pl
from jax.experimental.pallas import tpu as pltpu
import functools

courant = 0.4
vert_mix = 0.1
rotation = 0.3
buoyancy = 0.3
bottom_drag = 0.2


SIXTIETH = 1.0 / 60.0
INTERPRET = False
CENTRAL = {-2: 1.0, -1: -8.0, 0: 37.0, 1: 37.0, 2: -8.0, 3: 1.0}
DAMPING = {-2: -1.0, -1: 5.0, 0: -10.0, 1: 10.0, 2: -5.0, 3: 1.0}


def shifted(x, step, axis):
    n = x.shape[axis]
    step = step % n
    if step == 0:
        return x
    return pltpu.roll(x, n - step, axis)


def wet_of(depth, k):
    return jnp.where(depth > k + 0.5, 1.0, 0.0)


def bottom_of(depth, k):
    return jnp.where(jnp.abs(depth - (k + 1.0)) < 0.5, 1.0, 0.0)


def face_terms(q, axis):
    m2 = shifted(q, -2, axis)
    m1 = shifted(q, -1, axis)
    p1 = shifted(q, 1, axis)
    p2 = shifted(q, 2, axis)
    p3 = shifted(q, 3, axis)
    central = (37.0 * (q + p1) - 8.0 * (m1 + p2) + (m2 + p3)) * SIXTIETH
    damping = (10.0 * (p1 - q) - 5.0 * (p2 - m1) + (p3 - m2)) * SIXTIETH
    return central, damping


def face_speed(wet, speed, axis):
    open_face = wet * shifted(wet, 1, axis)
    w = 0.5 * (speed + shifted(speed, 1, axis))
    s = jnp.sqrt(w * w + 0.0001)
    return open_face, w, s


def forward(src, store, depth, cor):
    level_count = src.shape[1]
    column = None
    for k in range(level_count):
        wet = wet_of(depth, k)
        bottom = bottom_of(depth, k)
        q = [src[f, k] for f in range(4)]
        density = (-0.2 * q[0] + 0.8 * q[1]) * wet
        column = density if column is None else column + density
        pressure = buoyancy * column
        div = [None] * 4
        for axis, speed in ((1, q[2]), (0, q[3])):
            open_face, w, s = face_speed(wet, speed, axis)
            for f in range(4):
                central, damping = face_terms(q[f], axis)
                flux = open_face * (w * central - s * damping)
                part = flux - shifted(flux, -1, axis)
                div[f] = part if div[f] is None else div[f] + part
        press_east = 0.5 * (shifted(pressure, 1, 1) - shifted(pressure, -1, 1))
        press_north = 0.5 * (shifted(pressure, 1, 0) - shifted(pressure, -1, 0))
        force = [
            None,
            None,
            cor * q[3] - press_east - bottom_drag * bottom * q[2],
            -cor * q[2] - press_north - bottom_drag * bottom * q[3],
        ]
        for f in range(4):
            vertical = None
            if k > 0:
                vertical = wet_of(depth, k - 1) * (src[f, k - 1] - q[f])
            if k < level_count - 1:
                below = wet_of(depth, k + 1) * (src[f, k + 1] - q[f])
                vertical = below if vertical is None else vertical + below
            value = q[f] - courant * div[f] + vert_mix * vertical
            if force[f] is not None:
                value = value + force[f]
            store(f, k, value * wet)


def backward(x, lam, store, g_ref, depth, cor):
    level_count = x.shape[1]
    for k in range(level_count):
        wet = wet_of(depth, k)
        for f in range(4):
            g_ref[f, k] = wet * lam[f, k]
    density_bar = [None] * level_count
    column = None
    for k in reversed(range(level_count)):
        gu = g_ref[2, k]
        gv = g_ref[3, k]
        pbar = 0.5 * (shifted(gu, 1, 1) - shifted(gu, -1, 1)) + 0.5 * (
            shifted(gv, 1, 0) - shifted(gv, -1, 0)
        )
        column = pbar if column is None else column + pbar
        density_bar[k] = buoyancy * column
    for k in range(level_count):
        wet = wet_of(depth, k)
        bottom = bottom_of(depth, k)
        q = [x[f, k] for f in range(4)]
        g = [g_ref[f, k] for f in range(4)]
        acc = list(g)
        for f in range(4):
            vertical = None
            if k > 0:
                vertical = wet * g_ref[f, k - 1] - wet_of(depth, k - 1) * g[f]
            if k < level_count - 1:
                below = wet * g_ref[f, k + 1] - wet_of(depth, k + 1) * g[f]
                vertical = below if vertical is None else vertical + below
            acc[f] = acc[f] + vert_mix * vertical
        acc[2] = acc[2] - bottom_drag * bottom * g[2] - cor * g[3]
        acc[3] = acc[3] + cor * g[2] - bottom_drag * bottom * g[3]
        acc[0] = acc[0] - 0.2 * wet * density_bar[k]
        acc[1] = acc[1] + 0.8 * wet * density_bar[k]
        div_bar = [-courant * g[f] for f in range(4)]
        for axis, speed_field in ((1, 2), (0, 3)):
            open_face, w, s = face_speed(wet, q[speed_field], axis)
            ratio = w / s
            w_bar = None
            for f in range(4):
                flux_bar = open_face * (div_bar[f] - shifted(div_bar[f], 1, axis))
                central, damping = face_terms(q[f], axis)
                part = flux_bar * (central - ratio * damping)
                w_bar = part if w_bar is None else w_bar + part
                alpha = flux_bar * w * SIXTIETH
                beta = -flux_bar * s * SIXTIETH
                for j in range(-2, 4):
                    acc[f] = acc[f] + shifted(CENTRAL[j] * alpha + DAMPING[j] * beta, -j, axis)
            acc[speed_field] = acc[speed_field] + 0.5 * (w_bar + shifted(w_bar, -1, axis))
        for f in range(4):
            store(f, k, acc[f])


def assemble(dst, own, south, north, east, west, lane_pos, rowmask):
    rows, cols = own.shape
    depth = south.shape[0]
    frame_rows = dst.shape[0]
    dst[...] = jnp.zeros(dst.shape, jnp.float32)
    dst[0:rows, 0:cols] = own
    dst[rows : rows + depth, 0:cols] = south
    dst[frame_rows - depth : frame_rows, 0:cols] = north
    lane = lax.broadcasted_iota(jnp.int32, (frame_rows, 128), 1)
    from_east = shifted(east, lane_pos, 1)[:, 0:128]
    from_west = shifted(west, lane_pos - 116, 1)[:, 0:128]
    dst[:, cols : cols + 128] = jnp.where(lane < 12, from_east, jnp.where(lane >= 116, from_west, 0.0))
    dst[...] = dst[...] * rowmask


def two_step_kernel(
    margin, reach, own_x, own_c, own_d, north, south, west, east, rowmask_ref, cor_ref,
    final_ref, grad_ref, x0, lam, x1, mu, g_ref, depth_ref,
):
    fields, level_count, rows, cols = own_x.shape
    planes = fields * level_count
    frame_rows = x0.shape[2]
    rowmask = jnp.broadcast_to(rowmask_ref[...], (frame_rows, x0.shape[3]))
    cor = jnp.broadcast_to(cor_ref[...], (frame_rows, x0.shape[3]))
    east_msg = east[...]
    west_msg = west[...]
    for f in range(fields):
        for k in range(level_count):
            p = f * level_count + k
            assemble(
                x0.at[f, k], own_x[f, k], south[margin * p : margin * (p + 1), :],
                north[margin * p : margin * (p + 1), :], east_msg, west_msg, 12 * p, rowmask,
            )
    assemble(
        depth_ref, own_d[...], south[margin * planes : margin * (planes + 1), :],
        north[margin * planes : margin * (planes + 1), :], east_msg, west_msg, 12 * planes, rowmask,
    )
    base = margin * (planes + 1)
    for f in range(fields):
        for k in range(level_count):
            p = f * level_count + k
            assemble(
                lam.at[f, k], own_c[f, k], south[base + reach * p : base + reach * (p + 1), :],
                north[base + reach * p : base + reach * (p + 1), :], east_msg, west_msg,
                12 * (planes + 1 + p), rowmask,
            )
    depth = depth_ref[...]

    def keep(ref):
        def put(f, k, value):
            ref[f, k] = value
        return put

    def keep_cropped(ref):
        def put(f, k, value):
            ref[f, k] = value[:rows, :cols]
        return put

    forward(x0, keep(x1), depth, cor)
    forward(x1, keep_cropped(final_ref), depth, cor)
    backward(x1, lam, keep(mu), g_ref, depth, cor)
    backward(x0, mu, keep_cropped(grad_ref), g_ref, depth, cor)


def ring(count, step):
    return [(i, (i + step) % count) for i in range(count)]


def shards(state, cotangent, seamask, levels):
    fields, level_count, row_count, col_count = state.shape
    lat_total = row_count * lax.axis_size("lat")
    lat_start = lax.axis_index("lat") * row_count
    margin = 12
    reach = 6
    planes = fields * level_count
    depth = (seamask * levels).astype(jnp.float32)
    stacked = jnp.concatenate([state.reshape(planes, row_count, col_count), depth[None]], axis=0)
    cot = cotangent.reshape(planes, row_count, col_count)

    def lat_message(take_last):
        a = stacked[:, row_count - margin :, :] if take_last else stacked[:, :margin, :]
        c = cot[:, row_count - reach :, :] if take_last else cot[:, :reach, :]
        return jnp.concatenate([a.reshape(-1, col_count), c.reshape(-1, col_count)], axis=0)

    lat_count = lax.axis_size("lat")
    north = lax.ppermute(lat_message(True), "lat", ring(lat_count, 1))
    south = lax.ppermute(lat_message(False), "lat", ring(lat_count, -1))
    split = (planes + 1) * margin
    frame_rows = row_count + 2 * margin
    frame_cols = -(-(col_count + 2 * margin) // 128) * 128
    msg_cols = -(-(12 * (2 * planes + 1)) // 128) * 128

    def lon_message(take_last):
        lo, hi = (col_count - 12, col_count) if take_last else (0, 12)
        a = jnp.concatenate(
            [
                stacked[:, :, lo:hi],
                south[:split, lo:hi].reshape(planes + 1, margin, 12),
                north[:split, lo:hi].reshape(planes + 1, margin, 12),
            ],
            axis=1,
        )
        c = jnp.concatenate(
            [
                cot[:, :, lo:hi],
                south[split:, lo:hi].reshape(planes, reach, 12),
                jnp.zeros((planes, 2 * (margin - reach), 12), jnp.float32),
                north[split:, lo:hi].reshape(planes, reach, 12),
            ],
            axis=1,
        )
        m = jnp.transpose(jnp.concatenate([a, c], axis=0), (1, 0, 2)).reshape(frame_rows, -1)
        return jnp.pad(m, ((0, 0), (0, msg_cols - m.shape[1])))

    lon_count = lax.axis_size("lon")
    west = lax.ppermute(lon_message(True), "lon", ring(lon_count, 1))
    east = lax.ppermute(lon_message(False), "lon", ring(lon_count, -1))
    frame_index = jnp.arange(frame_rows, dtype=jnp.int32)
    global_row = lat_start + jnp.where(frame_index < row_count + margin, frame_index, frame_index - frame_rows)
    rowmask = ((global_row >= 0) & (global_row < lat_total)).astype(jnp.float32)[:, None]
    latitude = jnp.pi * ((global_row.astype(jnp.float32) + 0.5) / lat_total - 0.5)
    cor = (rotation * jnp.sin(latitude))[:, None]
    frame = (fields, level_count, frame_rows, frame_cols)
    out_block = jax.ShapeDtypeStruct((fields, level_count, row_count, col_count), jnp.float32)
    vmem = pl.BlockSpec(memory_space=pltpu.VMEM)
    final_state, adjoint_state = pl.pallas_call(
        functools.partial(two_step_kernel, margin, reach),
        out_shape=(out_block, out_block),
        in_specs=[vmem] * 9,
        out_specs=(vmem, vmem),
        scratch_shapes=[pltpu.VMEM(frame, jnp.float32) for _ in range(5)]
        + [pltpu.VMEM((frame_rows, frame_cols), jnp.float32)],
        interpret=INTERPRET,
    )(state, cotangent, depth, north, south, west, east, rowmask, cor)
    return (final_state, adjoint_state)


def solution(mesh):
    placed = (
        P(None, None, "lat", "lon"),
        P(None, None, "lat", "lon"),
        P("lat", "lon"),
        P("lat", "lon"),
    )
    return jax.shard_map(
        shards,
        mesh=mesh,
        in_specs=placed,
        out_specs=(P(None, None, "lat", "lon"), P(None, None, "lat", "lon")),
        check_vma=False,
    )
```

```python
import jax
import jax.numpy as jnp
from jax import lax
from jax.sharding import PartitionSpec as P
from jax.experimental import pallas as pl
from jax.experimental.pallas import tpu as pltpu
import functools

courant = 0.4
vert_mix = 0.1
rotation = 0.3
buoyancy = 0.3
bottom_drag = 0.2


SIXTIETH = 1.0 / 60.0
INTERPRET = False
CENTRAL = {-2: 1.0, -1: -8.0, 0: 37.0, 1: 37.0, 2: -8.0, 3: 1.0}
DAMPING = {-2: -1.0, -1: 5.0, 0: -10.0, 1: 10.0, 2: -5.0, 3: 1.0}


def shifted(x, step, axis):
    n = x.shape[axis]
    step = step % n
    if step == 0:
        return x
    return pltpu.roll(x, n - step, axis)


def wet_of(depth, k):
    return jnp.where(depth > k + 0.5, 1.0, 0.0)


def bottom_of(depth, k):
    return jnp.where(jnp.abs(depth - (k + 1.0)) < 0.5, 1.0, 0.0)


def face_terms(q, axis):
    m2 = shifted(q, -2, axis)
    m1 = shifted(q, -1, axis)
    p1 = shifted(q, 1, axis)
    p2 = shifted(q, 2, axis)
    p3 = shifted(q, 3, axis)
    central = (37.0 * (q + p1) - 8.0 * (m1 + p2) + (m2 + p3)) * SIXTIETH
    damping = (10.0 * (p1 - q) - 5.0 * (p2 - m1) + (p3 - m2)) * SIXTIETH
    return central, damping


def face_speed(wet, speed, axis):
    open_face = wet * shifted(wet, 1, axis)
    w = 0.5 * (speed + shifted(speed, 1, axis))
    s = jnp.sqrt(w * w + 0.0001)
    return open_face, w, s


def forward(src, store, depth, cor):
    level_count = src.shape[1]
    column = None
    for k in range(level_count):
        wet = wet_of(depth, k)
        bottom = bottom_of(depth, k)
        q = [src[f, k] for f in range(4)]
        density = (-0.2 * q[0] + 0.8 * q[1]) * wet
        column = density if column is None else column + density
        pressure = buoyancy * column
        div = [None] * 4
        for axis, speed in ((1, q[2]), (0, q[3])):
            open_face, w, s = face_speed(wet, speed, axis)
            for f in range(4):
                central, damping = face_terms(q[f], axis)
                flux = open_face * (w * central - s * damping)
                part = flux - shifted(flux, -1, axis)
                div[f] = part if div[f] is None else div[f] + part
        press_east = 0.5 * (shifted(pressure, 1, 1) - shifted(pressure, -1, 1))
        press_north = 0.5 * (shifted(pressure, 1, 0) - shifted(pressure, -1, 0))
        force = [
            None,
            None,
            cor * q[3] - press_east - bottom_drag * bottom * q[2],
            -cor * q[2] - press_north - bottom_drag * bottom * q[3],
        ]
        for f in range(4):
            vertical = None
            if k > 0:
                vertical = wet_of(depth, k - 1) * (src[f, k - 1] - q[f])
            if k < level_count - 1:
                below = wet_of(depth, k + 1) * (src[f, k + 1] - q[f])
                vertical = below if vertical is None else vertical + below
            value = q[f] - courant * div[f] + vert_mix * vertical
            if force[f] is not None:
                value = value + force[f]
            store(f, k, value * wet)


def backward(x, lam, store, g_ref, depth, cor):
    level_count = x.shape[1]
    for k in range(level_count):
        wet = wet_of(depth, k)
        for f in range(4):
            g_ref[f, k] = wet * lam[f, k]
    density_bar = [None] * level_count
    column = None
    for k in reversed(range(level_count)):
        gu = g_ref[2, k]
        gv = g_ref[3, k]
        pbar = 0.5 * (shifted(gu, 1, 1) - shifted(gu, -1, 1)) + 0.5 * (
            shifted(gv, 1, 0) - shifted(gv, -1, 0)
        )
        column = pbar if column is None else column + pbar
        density_bar[k] = buoyancy * column
    for k in range(level_count):
        wet = wet_of(depth, k)
        bottom = bottom_of(depth, k)
        q = [x[f, k] for f in range(4)]
        g = [g_ref[f, k] for f in range(4)]
        acc = list(g)
        for f in range(4):
            vertical = None
            if k > 0:
                vertical = wet * g_ref[f, k - 1] - wet_of(depth, k - 1) * g[f]
            if k < level_count - 1:
                below = wet * g_ref[f, k + 1] - wet_of(depth, k + 1) * g[f]
                vertical = below if vertical is None else vertical + below
            acc[f] = acc[f] + vert_mix * vertical
        acc[2] = acc[2] - bottom_drag * bottom * g[2] - cor * g[3]
        acc[3] = acc[3] + cor * g[2] - bottom_drag * bottom * g[3]
        acc[0] = acc[0] - 0.2 * wet * density_bar[k]
        acc[1] = acc[1] + 0.8 * wet * density_bar[k]
        div_bar = [-courant * g[f] for f in range(4)]
        for axis, speed_field in ((1, 2), (0, 3)):
            open_face, w, s = face_speed(wet, q[speed_field], axis)
            ratio = w / s
            w_bar = None
            for f in range(4):
                flux_bar = open_face * (div_bar[f] - shifted(div_bar[f], 1, axis))
                central, damping = face_terms(q[f], axis)
                part = flux_bar * (central - ratio * damping)
                w_bar = part if w_bar is None else w_bar + part
                alpha = flux_bar * w * SIXTIETH
                beta = -flux_bar * s * SIXTIETH
                for j in range(-2, 4):
                    acc[f] = acc[f] + shifted(CENTRAL[j] * alpha + DAMPING[j] * beta, -j, axis)
            acc[speed_field] = acc[speed_field] + 0.5 * (w_bar + shifted(w_bar, -1, axis))
        for f in range(4):
            store(f, k, acc[f])


def strip_place(p):
    return p // 10, 12 * (p % 10)


def assemble(dst, own, south, north, east, west, p, rowmask):
    rows, cols = own.shape
    depth = south.shape[0]
    frame_rows = dst.shape[0]
    dst[...] = jnp.zeros(dst.shape, jnp.float32)
    dst[0:rows, 0:cols] = own
    dst[rows : rows + depth, 0:cols] = south
    dst[frame_rows - depth : frame_rows, 0:cols] = north
    lane = lax.broadcasted_iota(jnp.int32, (frame_rows, 128), 1)
    block, offset = strip_place(p)
    from_east = shifted(east[:, 128 * block : 128 * (block + 1)], offset, 1)
    from_west = shifted(west[:, 128 * block : 128 * (block + 1)], offset - 116, 1)
    dst[:, cols : cols + 128] = jnp.where(lane < 12, from_east, jnp.where(lane >= 116, from_west, 0.0))
    dst[...] = dst[...] * rowmask


def two_step_kernel(
    margin, reach, own_x, own_c, own_d, north, south, west, east, rowmask_ref, cor_ref,
    final_ref, grad_ref, x0, lam, x1, mu, g_ref, depth_ref,
):
    fields, level_count, rows, cols = own_x.shape
    planes = fields * level_count
    frame_rows = x0.shape[2]
    rowmask = jnp.broadcast_to(rowmask_ref[...], (frame_rows, x0.shape[3]))
    cor = jnp.broadcast_to(cor_ref[...], (frame_rows, x0.shape[3]))
    east_msg = east[...]
    west_msg = west[...]
    for f in range(fields):
        for k in range(level_count):
            p = f * level_count + k
            assemble(
                x0.at[f, k], own_x[f, k], south[margin * p : margin * (p + 1), :],
                north[margin * p : margin * (p + 1), :], east_msg, west_msg, p, rowmask,
            )
    assemble(
        depth_ref, own_d[...], south[margin * planes : margin * (planes + 1), :],
        north[margin * planes : margin * (planes + 1), :], east_msg, west_msg, planes, rowmask,
    )
    base = margin * (planes + 1)
    for f in range(fields):
        for k in range(level_count):
            p = f * level_count + k
            assemble(
                lam.at[f, k], own_c[f, k], south[base + reach * p : base + reach * (p + 1), :],
                north[base + reach * p : base + reach * (p + 1), :], east_msg, west_msg,
                planes + 1 + p, rowmask,
            )
    depth = depth_ref[...]

    def keep(ref):
        def put(f, k, value):
            ref[f, k] = value
        return put

    def keep_cropped(ref):
        def put(f, k, value):
            ref[f, k] = value[:rows, :cols]
        return put

    forward(x0, keep(x1), depth, cor)
    forward(x1, keep_cropped(final_ref), depth, cor)
    backward(x1, lam, keep(mu), g_ref, depth, cor)
    backward(x0, mu, keep_cropped(grad_ref), g_ref, depth, cor)


def lat_pack_kernel(margin, reach, own_x, own_c, own_d, north_msg, south_msg):
    fields, level_count, rows, cols = own_x.shape
    planes = fields * level_count
    for f in range(fields):
        for k in range(level_count):
            p = f * level_count + k
            north_msg[margin * p : margin * (p + 1), :] = own_x[f, k, rows - margin : rows, :]
            south_msg[margin * p : margin * (p + 1), :] = own_x[f, k, 0:margin, :]
    north_msg[margin * planes : margin * (planes + 1), :] = own_d[rows - margin : rows, :]
    south_msg[margin * planes : margin * (planes + 1), :] = own_d[0:margin, :]
    base = margin * (planes + 1)
    for f in range(fields):
        for k in range(level_count):
            p = f * level_count + k
            north_msg[base + reach * p : base + reach * (p + 1), :] = own_c[f, k, rows - reach : rows, :]
            south_msg[base + reach * p : base + reach * (p + 1), :] = own_c[f, k, 0:reach, :]


def lon_pack_kernel(margin, reach, own_x, own_c, own_d, north, south, west_msg, east_msg, ext):
    fields, level_count, rows, cols = own_x.shape
    planes = fields * level_count
    frame_rows = ext.shape[0]
    lane = lax.broadcasted_iota(jnp.int32, (frame_rows, 128), 1)
    west_acc = [jnp.zeros((frame_rows, 128), jnp.float32) for _ in range(west_msg.shape[1] // 128)]
    east_acc = [jnp.zeros((frame_rows, 128), jnp.float32) for _ in range(east_msg.shape[1] // 128)]

    def add_plane(p, own, south_rows, north_rows):
        depth = south_rows.shape[0]
        ext[...] = jnp.zeros(ext.shape, jnp.float32)
        ext[0:rows, :] = own
        ext[rows : rows + depth, :] = south_rows
        ext[frame_rows - depth : frame_rows, :] = north_rows
        block, offset = strip_place(p)
        keep = (lane >= offset) & (lane < offset + 12)
        last = shifted(ext[:, cols - 128 : cols], 116 - offset, 1)
        first = shifted(ext[:, 0:128], -offset, 1)
        west_acc[block] = west_acc[block] + jnp.where(keep, last, 0.0)
        east_acc[block] = east_acc[block] + jnp.where(keep, first, 0.0)

    for f in range(fields):
        for k in range(level_count):
            p = f * level_count + k
            add_plane(p, own_x[f, k], south[margin * p : margin * (p + 1), :], north[margin * p : margin * (p + 1), :])
    add_plane(
        planes, own_d[...], south[margin * planes : margin * (planes + 1), :],
        north[margin * planes : margin * (planes + 1), :],
    )
    base = margin * (planes + 1)
    for f in range(fields):
        for k in range(level_count):
            p = f * level_count + k
            add_plane(
                planes + 1 + p, own_c[f, k], south[base + reach * p : base + reach * (p + 1), :],
                north[base + reach * p : base + reach * (p + 1), :],
            )
    for block in range(len(west_acc)):
        west_msg[:, 128 * block : 128 * (block + 1)] = west_acc[block]
        east_msg[:, 128 * block : 128 * (block + 1)] = east_acc[block]


def ring(count, step):
    return [(i, (i + step) % count) for i in range(count)]


def shards(state, cotangent, seamask, levels):
    fields, level_count, row_count, col_count = state.shape
    lat_total = row_count * lax.axis_size("lat")
    lat_start = lax.axis_index("lat") * row_count
    margin = 12
    reach = 6
    planes = fields * level_count
    depth = (seamask * levels).astype(jnp.float32)
    vmem = pl.BlockSpec(memory_space=pltpu.VMEM)
    msg_rows = (planes + 1) * margin + planes * reach
    lat_msg = jax.ShapeDtypeStruct((msg_rows, col_count), jnp.float32)
    north_out, south_out = pl.pallas_call(
        functools.partial(lat_pack_kernel, margin, reach),
        out_shape=(lat_msg, lat_msg),
        in_specs=[vmem] * 3,
        out_specs=(vmem, vmem),
        interpret=INTERPRET,
    )(state, cotangent, depth)
    lat_count = lax.axis_size("lat")
    north = lax.ppermute(north_out, "lat", ring(lat_count, 1))
    south = lax.ppermute(south_out, "lat", ring(lat_count, -1))
    frame_rows = row_count + 2 * margin
    frame_cols = -(-(col_count + 2 * margin) // 128) * 128
    msg_cols = 128 * (-(-(2 * planes + 1) // 10))
    lon_msg = jax.ShapeDtypeStruct((frame_rows, msg_cols), jnp.float32)
    west_out, east_out = pl.pallas_call(
        functools.partial(lon_pack_kernel, margin, reach),
        out_shape=(lon_msg, lon_msg),
        in_specs=[vmem] * 5,
        out_specs=(vmem, vmem),
        scratch_shapes=[pltpu.VMEM((frame_rows, col_count), jnp.float32)],
        interpret=INTERPRET,
    )(state, cotangent, depth, north, south)
    lon_count = lax.axis_size("lon")
    west = lax.ppermute(west_out, "lon", ring(lon_count, 1))
    east = lax.ppermute(east_out, "lon", ring(lon_count, -1))
    frame_index = jnp.arange(frame_rows, dtype=jnp.int32)
    global_row = lat_start + jnp.where(frame_index < row_count + margin, frame_index, frame_index - frame_rows)
    rowmask = ((global_row >= 0) & (global_row < lat_total)).astype(jnp.float32)[:, None]
    latitude = jnp.pi * ((global_row.astype(jnp.float32) + 0.5) / lat_total - 0.5)
    cor = (rotation * jnp.sin(latitude))[:, None]
    frame = (fields, level_count, frame_rows, frame_cols)
    out_block = jax.ShapeDtypeStruct((fields, level_count, row_count, col_count), jnp.float32)
    final_state, adjoint_state = pl.pallas_call(
        functools.partial(two_step_kernel, margin, reach),
        out_shape=(out_block, out_block),
        in_specs=[vmem] * 9,
        out_specs=(vmem, vmem),
        scratch_shapes=[pltpu.VMEM(frame, jnp.float32) for _ in range(5)]
        + [pltpu.VMEM((frame_rows, frame_cols), jnp.float32)],
        interpret=INTERPRET,
    )(state, cotangent, depth, north, south, west, east, rowmask, cor)
    return (final_state, adjoint_state)


def solution(mesh):
    placed = (
        P(None, None, "lat", "lon"),
        P(None, None, "lat", "lon"),
        P("lat", "lon"),
        P("lat", "lon"),
    )
    return jax.shard_map(
        shards,
        mesh=mesh,
        in_specs=placed,
        out_specs=(P(None, None, "lat", "lon"), P(None, None, "lat", "lon")),
        check_vma=False,
    )
```

```python
import jax
import jax.numpy as jnp
from jax import lax
from jax.sharding import PartitionSpec as P
from jax.experimental import pallas as pl
from jax.experimental.pallas import tpu as pltpu
import functools

courant = 0.4
vert_mix = 0.1
rotation = 0.3
buoyancy = 0.3
bottom_drag = 0.2


SIXTIETH = 1.0 / 60.0
INTERPRET = False
CENTRAL = {-2: 1.0, -1: -8.0, 0: 37.0, 1: 37.0, 2: -8.0, 3: 1.0}
DAMPING = {-2: -1.0, -1: 5.0, 0: -10.0, 1: 10.0, 2: -5.0, 3: 1.0}


def shifted(x, step, axis):
    n = x.shape[axis]
    step = step % n
    if step == 0:
        return x
    return pltpu.roll(x, n - step, axis)


def wet_of(depth, k):
    return jnp.where(depth > k + 0.5, 1.0, 0.0)


def bottom_of(depth, k):
    return jnp.where(jnp.abs(depth - (k + 1.0)) < 0.5, 1.0, 0.0)


def face_terms(q, axis):
    m2 = shifted(q, -2, axis)
    m1 = shifted(q, -1, axis)
    p1 = shifted(q, 1, axis)
    p2 = shifted(q, 2, axis)
    p3 = shifted(q, 3, axis)
    central = (37.0 * (q + p1) - 8.0 * (m1 + p2) + (m2 + p3)) * SIXTIETH
    damping = (10.0 * (p1 - q) - 5.0 * (p2 - m1) + (p3 - m2)) * SIXTIETH
    return central, damping


def face_speed(wet, speed, axis):
    open_face = wet * shifted(wet, 1, axis)
    w = 0.5 * (speed + shifted(speed, 1, axis))
    s = jnp.sqrt(w * w + 0.0001)
    return open_face, w, s


def forward(src, store, depth, cor, terms):
    level_count = src.shape[1]
    column = None
    for k in range(level_count):
        wet = wet_of(depth, k)
        bottom = bottom_of(depth, k)
        q = [src[f, k] for f in range(4)]
        density = (-0.2 * q[0] + 0.8 * q[1]) * wet
        column = density if column is None else column + density
        pressure = buoyancy * column
        div = [None] * 4
        for d, (axis, speed) in enumerate(((1, q[2]), (0, q[3]))):
            open_face, w, s = face_speed(wet, speed, axis)
            ratio = w / s
            for f in range(4):
                central, damping = face_terms(q[f], axis)
                terms[d, f, k] = central - ratio * damping
                flux = open_face * (w * central - s * damping)
                part = flux - shifted(flux, -1, axis)
                div[f] = part if div[f] is None else div[f] + part
        press_east = 0.5 * (shifted(pressure, 1, 1) - shifted(pressure, -1, 1))
        press_north = 0.5 * (shifted(pressure, 1, 0) - shifted(pressure, -1, 0))
        force = [
            None,
            None,
            cor * q[3] - press_east - bottom_drag * bottom * q[2],
            -cor * q[2] - press_north - bottom_drag * bottom * q[3],
        ]
        for f in range(4):
            vertical = None
            if k > 0:
                vertical = wet_of(depth, k - 1) * (src[f, k - 1] - q[f])
            if k < level_count - 1:
                below = wet_of(depth, k + 1) * (src[f, k + 1] - q[f])
                vertical = below if vertical is None else vertical + below
            value = q[f] - courant * div[f] + vert_mix * vertical
            if force[f] is not None:
                value = value + force[f]
            store(f, k, value * wet)


def backward(x, lam, store, g_ref, depth, cor, terms):
    level_count = x.shape[1]
    for k in range(level_count):
        wet = wet_of(depth, k)
        for f in range(4):
            g_ref[f, k] = wet * lam[f, k]
    density_bar = [None] * level_count
    column = None
    for k in reversed(range(level_count)):
        gu = g_ref[2, k]
        gv = g_ref[3, k]
        pbar = 0.5 * (shifted(gu, 1, 1) - shifted(gu, -1, 1)) + 0.5 * (
            shifted(gv, 1, 0) - shifted(gv, -1, 0)
        )
        column = pbar if column is None else column + pbar
        density_bar[k] = buoyancy * column
    for k in range(level_count):
        wet = wet_of(depth, k)
        bottom = bottom_of(depth, k)
        q = [x[f, k] for f in range(4)]
        g = [g_ref[f, k] for f in range(4)]
        acc = list(g)
        for f in range(4):
            vertical = None
            if k > 0:
                vertical = wet * g_ref[f, k - 1] - wet_of(depth, k - 1) * g[f]
            if k < level_count - 1:
                below = wet * g_ref[f, k + 1] - wet_of(depth, k + 1) * g[f]
                vertical = below if vertical is None else vertical + below
            acc[f] = acc[f] + vert_mix * vertical
        acc[2] = acc[2] - bottom_drag * bottom * g[2] - cor * g[3]
        acc[3] = acc[3] + cor * g[2] - bottom_drag * bottom * g[3]
        acc[0] = acc[0] - 0.2 * wet * density_bar[k]
        acc[1] = acc[1] + 0.8 * wet * density_bar[k]
        div_bar = [-courant * g[f] for f in range(4)]
        for d, (axis, speed_field) in enumerate(((1, 2), (0, 3))):
            open_face, w, s = face_speed(wet, q[speed_field], axis)
            w_bar = None
            for f in range(4):
                flux_bar = open_face * (div_bar[f] - shifted(div_bar[f], 1, axis))
                part = flux_bar * terms[d, f, k]
                w_bar = part if w_bar is None else w_bar + part
                alpha = flux_bar * w * SIXTIETH
                beta = -flux_bar * s * SIXTIETH
                for j in range(-2, 4):
                    acc[f] = acc[f] + shifted(CENTRAL[j] * alpha + DAMPING[j] * beta, -j, axis)
            acc[speed_field] = acc[speed_field] + 0.5 * (w_bar + shifted(w_bar, -1, axis))
        for f in range(4):
            store(f, k, acc[f])


def strip_place(p):
    return p // 10, 12 * (p % 10)


def assemble(dst, own, south, north, east, west, p, rowmask):
    rows, cols = own.shape
    depth = south.shape[0]
    frame_rows = dst.shape[0]
    dst[...] = jnp.zeros(dst.shape, jnp.float32)
    dst[0:rows, 0:cols] = own
    dst[rows : rows + depth, 0:cols] = south
    dst[frame_rows - depth : frame_rows, 0:cols] = north
    lane = lax.broadcasted_iota(jnp.int32, (frame_rows, 128), 1)
    block, offset = strip_place(p)
    from_east = shifted(east[:, 128 * block : 128 * (block + 1)], offset, 1)
    from_west = shifted(west[:, 128 * block : 128 * (block + 1)], offset - 116, 1)
    dst[:, cols : cols + 128] = jnp.where(lane < 12, from_east, jnp.where(lane >= 116, from_west, 0.0))
    dst[...] = dst[...] * rowmask


def two_step_kernel(
    margin, reach, own_x, own_c, own_d, north, south, west, east, rowmask_ref, cor_ref,
    final_ref, grad_ref, x0, lam, x1, mu, g_ref, depth_ref, terms_first, terms_second,
):
    fields, level_count, rows, cols = own_x.shape
    planes = fields * level_count
    frame_rows = x0.shape[2]
    rowmask = jnp.broadcast_to(rowmask_ref[...], (frame_rows, x0.shape[3]))
    cor = jnp.broadcast_to(cor_ref[...], (frame_rows, x0.shape[3]))
    east_msg = east[...]
    west_msg = west[...]
    for f in range(fields):
        for k in range(level_count):
            p = f * level_count + k
            assemble(
                x0.at[f, k], own_x[f, k], south[margin * p : margin * (p + 1), :],
                north[margin * p : margin * (p + 1), :], east_msg, west_msg, p, rowmask,
            )
    assemble(
        depth_ref, own_d[...], south[margin * planes : margin * (planes + 1), :],
        north[margin * planes : margin * (planes + 1), :], east_msg, west_msg, planes, rowmask,
    )
    base = margin * (planes + 1)
    for f in range(fields):
        for k in range(level_count):
            p = f * level_count + k
            assemble(
                lam.at[f, k], own_c[f, k], south[base + reach * p : base + reach * (p + 1), :],
                north[base + reach * p : base + reach * (p + 1), :], east_msg, west_msg,
                planes + 1 + p, rowmask,
            )
    depth = depth_ref[...]

    def keep(ref):
        def put(f, k, value):
            ref[f, k] = value
        return put

    def keep_cropped(ref):
        def put(f, k, value):
            ref[f, k] = value[:rows, :cols]
        return put

    forward(x0, keep(x1), depth, cor, terms_first)
    forward(x1, keep_cropped(final_ref), depth, cor, terms_second)
    backward(x1, lam, keep(mu), g_ref, depth, cor, terms_second)
    backward(x0, mu, keep_cropped(grad_ref), g_ref, depth, cor, terms_first)


def lat_pack_kernel(margin, reach, own_x, own_c, sea_ref, level_ref, north_msg, south_msg, own_d):
    fields, level_count, rows, cols = own_x.shape
    own_d[...] = (sea_ref[...] * level_ref[...]).astype(jnp.float32)
    planes = fields * level_count
    for f in range(fields):
        for k in range(level_count):
            p = f * level_count + k
            north_msg[margin * p : margin * (p + 1), :] = own_x[f, k, rows - margin : rows, :]
            south_msg[margin * p : margin * (p + 1), :] = own_x[f, k, 0:margin, :]
    north_msg[margin * planes : margin * (planes + 1), :] = own_d[rows - margin : rows, :]
    south_msg[margin * planes : margin * (planes + 1), :] = own_d[0:margin, :]
    base = margin * (planes + 1)
    for f in range(fields):
        for k in range(level_count):
            p = f * level_count + k
            north_msg[base + reach * p : base + reach * (p + 1), :] = own_c[f, k, rows - reach : rows, :]
            south_msg[base + reach * p : base + reach * (p + 1), :] = own_c[f, k, 0:reach, :]


def lon_pack_kernel(margin, reach, own_x, own_c, own_d, north, south, west_msg, east_msg, ext):
    fields, level_count, rows, cols = own_x.shape
    planes = fields * level_count
    frame_rows = ext.shape[0]
    lane = lax.broadcasted_iota(jnp.int32, (frame_rows, 128), 1)
    west_acc = [jnp.zeros((frame_rows, 128), jnp.float32) for _ in range(west_msg.shape[1] // 128)]
    east_acc = [jnp.zeros((frame_rows, 128), jnp.float32) for _ in range(east_msg.shape[1] // 128)]

    def add_plane(p, own, south_rows, north_rows):
        depth = south_rows.shape[0]
        ext[...] = jnp.zeros(ext.shape, jnp.float32)
        ext[0:rows, :] = own
        ext[rows : rows + depth, :] = south_rows
        ext[frame_rows - depth : frame_rows, :] = north_rows
        block, offset = strip_place(p)
        keep = (lane >= offset) & (lane < offset + 12)
        last = shifted(ext[:, cols - 128 : cols], 116 - offset, 1)
        first = shifted(ext[:, 0:128], -offset, 1)
        west_acc[block] = west_acc[block] + jnp.where(keep, last, 0.0)
        east_acc[block] = east_acc[block] + jnp.where(keep, first, 0.0)

    for f in range(fields):
        for k in range(level_count):
            p = f * level_count + k
            add_plane(p, own_x[f, k], south[margin * p : margin * (p + 1), :], north[margin * p : margin * (p + 1), :])
    add_plane(
        planes, own_d[...], south[margin * planes : margin * (planes + 1), :],
        north[margin * planes : margin * (planes + 1), :],
    )
    base = margin * (planes + 1)
    for f in range(fields):
        for k in range(level_count):
            p = f * level_count + k
            add_plane(
                planes + 1 + p, own_c[f, k], south[base + reach * p : base + reach * (p + 1), :],
                north[base + reach * p : base + reach * (p + 1), :],
            )
    for block in range(len(west_acc)):
        west_msg[:, 128 * block : 128 * (block + 1)] = west_acc[block]
        east_msg[:, 128 * block : 128 * (block + 1)] = east_acc[block]


def ring(count, step):
    return [(i, (i + step) % count) for i in range(count)]


def shards(state, cotangent, seamask, levels):
    fields, level_count, row_count, col_count = state.shape
    lat_total = row_count * lax.axis_size("lat")
    lat_start = lax.axis_index("lat") * row_count
    margin = 12
    reach = 6
    planes = fields * level_count
    vmem = pl.BlockSpec(memory_space=pltpu.VMEM)
    msg_rows = (planes + 1) * margin + planes * reach
    lat_msg = jax.ShapeDtypeStruct((msg_rows, col_count), jnp.float32)
    north_out, south_out, depth = pl.pallas_call(
        functools.partial(lat_pack_kernel, margin, reach),
        out_shape=(lat_msg, lat_msg, jax.ShapeDtypeStruct((row_count, col_count), jnp.float32)),
        in_specs=[vmem] * 4,
        out_specs=(vmem, vmem, vmem),
        interpret=INTERPRET,
    )(state, cotangent, seamask, levels)
    lat_count = lax.axis_size("lat")
    north = lax.ppermute(north_out, "lat", ring(lat_count, 1))
    south = lax.ppermute(south_out, "lat", ring(lat_count, -1))
    frame_rows = row_count + 2 * margin
    frame_cols = -(-(col_count + 2 * margin) // 128) * 128
    msg_cols = 128 * (-(-(2 * planes + 1) // 10))
    lon_msg = jax.ShapeDtypeStruct((frame_rows, msg_cols), jnp.float32)
    west_out, east_out = pl.pallas_call(
        functools.partial(lon_pack_kernel, margin, reach),
        out_shape=(lon_msg, lon_msg),
        in_specs=[vmem] * 5,
        out_specs=(vmem, vmem),
        scratch_shapes=[pltpu.VMEM((frame_rows, col_count), jnp.float32)],
        interpret=INTERPRET,
    )(state, cotangent, depth, north, south)
    lon_count = lax.axis_size("lon")
    west = lax.ppermute(west_out, "lon", ring(lon_count, 1))
    east = lax.ppermute(east_out, "lon", ring(lon_count, -1))
    frame_index = jnp.arange(frame_rows, dtype=jnp.int32)
    global_row = lat_start + jnp.where(frame_index < row_count + margin, frame_index, frame_index - frame_rows)
    rowmask = ((global_row >= 0) & (global_row < lat_total)).astype(jnp.float32)[:, None]
    latitude = jnp.pi * ((global_row.astype(jnp.float32) + 0.5) / lat_total - 0.5)
    cor = (rotation * jnp.sin(latitude))[:, None]
    frame = (fields, level_count, frame_rows, frame_cols)
    out_block = jax.ShapeDtypeStruct((fields, level_count, row_count, col_count), jnp.float32)
    final_state, adjoint_state = pl.pallas_call(
        functools.partial(two_step_kernel, margin, reach),
        out_shape=(out_block, out_block),
        in_specs=[vmem] * 9,
        out_specs=(vmem, vmem),
        scratch_shapes=[pltpu.VMEM(frame, jnp.float32) for _ in range(5)]
        + [pltpu.VMEM((frame_rows, frame_cols), jnp.float32)]
        + [pltpu.VMEM((2,) + frame, jnp.float32) for _ in range(2)],
        interpret=INTERPRET,
    )(state, cotangent, depth, north, south, west, east, rowmask, cor)
    return (final_state, adjoint_state)


def solution(mesh):
    placed = (
        P(None, None, "lat", "lon"),
        P(None, None, "lat", "lon"),
        P("lat", "lon"),
        P("lat", "lon"),
    )
    return jax.shard_map(
        shards,
        mesh=mesh,
        in_specs=placed,
        out_specs=(P(None, None, "lat", "lon"), P(None, None, "lat", "lon")),
        check_vma=False,
    )
```

```python
import jax
import jax.numpy as jnp
from jax import lax
from jax.sharding import PartitionSpec as P
from jax.experimental import pallas as pl
from jax.experimental.pallas import tpu as pltpu
import functools

courant = 0.4
vert_mix = 0.1
rotation = 0.3
buoyancy = 0.3
bottom_drag = 0.2


SIXTIETH = 1.0 / 60.0
INTERPRET = False
CENTRAL = {-2: 1.0, -1: -8.0, 0: 37.0, 1: 37.0, 2: -8.0, 3: 1.0}
DAMPING = {-2: -1.0, -1: 5.0, 0: -10.0, 1: 10.0, 2: -5.0, 3: 1.0}


def shifted(x, step, axis):
    n = x.shape[axis]
    step = step % n
    if step == 0:
        return x
    return pltpu.roll(x, n - step, axis)


def wet_of(depth, k):
    return jnp.where(depth > k + 0.5, 1.0, 0.0)


def bottom_of(depth, k):
    return jnp.where(jnp.abs(depth - (k + 1.0)) < 0.5, 1.0, 0.0)


def face_terms(q, axis):
    m2 = shifted(q, -2, axis)
    m1 = shifted(q, -1, axis)
    p1 = shifted(q, 1, axis)
    p2 = shifted(q, 2, axis)
    p3 = shifted(q, 3, axis)
    central = 37.0 * (q + p1) - 8.0 * (m1 + p2) + (m2 + p3)
    damping = 10.0 * (p1 - q) - 5.0 * (p2 - m1) + (p3 - m2)
    return central, damping


def face_speed(wet, speed, axis):
    open_face = wet * shifted(wet, 1, axis)
    w = 0.5 * (speed + shifted(speed, 1, axis))
    s = jnp.sqrt(w * w + 0.0001)
    return open_face, w, s


def forward(src, store, depth, cor, terms):
    level_count = src.shape[1]
    column = None
    for k in range(level_count):
        wet = wet_of(depth, k)
        bottom = bottom_of(depth, k)
        q = [src[f, k] for f in range(4)]
        density = (-0.2 * q[0] + 0.8 * q[1]) * wet
        column = density if column is None else column + density
        pressure = buoyancy * column
        div = [None] * 4
        for d, (axis, speed) in enumerate(((1, q[2]), (0, q[3]))):
            open_face, w, s = face_speed(wet, speed, axis)
            ratio = w / s
            w = w * SIXTIETH
            s = s * SIXTIETH
            for f in range(4):
                central, damping = face_terms(q[f], axis)
                terms[d, f, k] = central - ratio * damping
                flux = open_face * (w * central - s * damping)
                part = flux - shifted(flux, -1, axis)
                div[f] = part if div[f] is None else div[f] + part
        press_east = 0.5 * (shifted(pressure, 1, 1) - shifted(pressure, -1, 1))
        press_north = 0.5 * (shifted(pressure, 1, 0) - shifted(pressure, -1, 0))
        force = [
            None,
            None,
            cor * q[3] - press_east - bottom_drag * bottom * q[2],
            -cor * q[2] - press_north - bottom_drag * bottom * q[3],
        ]
        for f in range(4):
            vertical = None
            if k > 0:
                vertical = wet_of(depth, k - 1) * (src[f, k - 1] - q[f])
            if k < level_count - 1:
                below = wet_of(depth, k + 1) * (src[f, k + 1] - q[f])
                vertical = below if vertical is None else vertical + below
            value = q[f] - courant * div[f] + vert_mix * vertical
            if force[f] is not None:
                value = value + force[f]
            store(f, k, value * wet)


def backward(x, lam, store, g_ref, depth, cor, terms):
    level_count = x.shape[1]
    for k in range(level_count):
        wet = wet_of(depth, k)
        for f in range(4):
            g_ref[f, k] = wet * lam[f, k]
    density_bar = [None] * level_count
    column = None
    for k in reversed(range(level_count)):
        gu = g_ref[2, k]
        gv = g_ref[3, k]
        pbar = 0.5 * (shifted(gu, 1, 1) - shifted(gu, -1, 1)) + 0.5 * (
            shifted(gv, 1, 0) - shifted(gv, -1, 0)
        )
        column = pbar if column is None else column + pbar
        density_bar[k] = buoyancy * column
    for k in range(level_count):
        wet = wet_of(depth, k)
        bottom = bottom_of(depth, k)
        q = [x[f, k] for f in range(4)]
        g = [g_ref[f, k] for f in range(4)]
        acc = list(g)
        for f in range(4):
            vertical = None
            if k > 0:
                vertical = wet * g_ref[f, k - 1] - wet_of(depth, k - 1) * g[f]
            if k < level_count - 1:
                below = wet * g_ref[f, k + 1] - wet_of(depth, k + 1) * g[f]
                vertical = below if vertical is None else vertical + below
            acc[f] = acc[f] + vert_mix * vertical
        acc[2] = acc[2] - bottom_drag * bottom * g[2] - cor * g[3]
        acc[3] = acc[3] + cor * g[2] - bottom_drag * bottom * g[3]
        acc[0] = acc[0] - 0.2 * wet * density_bar[k]
        acc[1] = acc[1] + 0.8 * wet * density_bar[k]
        div_bar = [-courant * g[f] for f in range(4)]
        for d, (axis, speed_field) in enumerate(((1, 2), (0, 3))):
            open_face, w, s = face_speed(wet, q[speed_field], axis)
            w = w * SIXTIETH
            s = s * SIXTIETH
            w_bar = None
            for f in range(4):
                flux_bar = open_face * (div_bar[f] - shifted(div_bar[f], 1, axis))
                part = flux_bar * terms[d, f, k]
                w_bar = part if w_bar is None else w_bar + part
                alpha = flux_bar * w
                beta = -flux_bar * s
                for j in range(-2, 4):
                    acc[f] = acc[f] + shifted(CENTRAL[j] * alpha + DAMPING[j] * beta, -j, axis)
            acc[speed_field] = acc[speed_field] + (0.5 * SIXTIETH) * (w_bar + shifted(w_bar, -1, axis))
        for f in range(4):
            store(f, k, acc[f])


def strip_place(p):
    return p // 10, 12 * (p % 10)


def assemble(dst, own, south, north, east, west, p, rowmask):
    rows, cols = own.shape
    depth = south.shape[0]
    frame_rows = dst.shape[0]
    dst[...] = jnp.zeros(dst.shape, jnp.float32)
    dst[0:rows, 0:cols] = own
    dst[rows : rows + depth, 0:cols] = south
    dst[frame_rows - depth : frame_rows, 0:cols] = north
    lane = lax.broadcasted_iota(jnp.int32, (frame_rows, 128), 1)
    block, offset = strip_place(p)
    from_east = shifted(east[:, 128 * block : 128 * (block + 1)], offset, 1)
    from_west = shifted(west[:, 128 * block : 128 * (block + 1)], offset - 116, 1)
    dst[:, cols : cols + 128] = jnp.where(lane < 12, from_east, jnp.where(lane >= 116, from_west, 0.0))
    dst[...] = dst[...] * rowmask


def two_step_kernel(
    margin, reach, own_x, own_c, own_d, north, south, west, east, rowmask_ref, cor_ref,
    final_ref, grad_ref, x0, lam, x1, mu, g_ref, depth_ref, terms_first, terms_second,
):
    fields, level_count, rows, cols = own_x.shape
    planes = fields * level_count
    frame_rows = x0.shape[2]
    rowmask = jnp.broadcast_to(rowmask_ref[...], (frame_rows, x0.shape[3]))
    cor = jnp.broadcast_to(cor_ref[...], (frame_rows, x0.shape[3]))
    east_msg = east[...]
    west_msg = west[...]
    for f in range(fields):
        for k in range(level_count):
            p = f * level_count + k
            assemble(
                x0.at[f, k], own_x[f, k], south[margin * p : margin * (p + 1), :],
                north[margin * p : margin * (p + 1), :], east_msg, west_msg, p, rowmask,
            )
    assemble(
        depth_ref, own_d[...], south[margin * planes : margin * (planes + 1), :],
        north[margin * planes : margin * (planes + 1), :], east_msg, west_msg, planes, rowmask,
    )
    base = margin * (planes + 1)
    for f in range(fields):
        for k in range(level_count):
            p = f * level_count + k
            assemble(
                lam.at[f, k], own_c[f, k], south[base + reach * p : base + reach * (p + 1), :],
                north[base + reach * p : base + reach * (p + 1), :], east_msg, west_msg,
                planes + 1 + p, rowmask,
            )
    depth = depth_ref[...]

    def keep(ref):
        def put(f, k, value):
            ref[f, k] = value
        return put

    def keep_cropped(ref):
        def put(f, k, value):
            ref[f, k] = value[:rows, :cols]
        return put

    forward(x0, keep(x1), depth, cor, terms_first)
    forward(x1, keep_cropped(final_ref), depth, cor, terms_second)
    backward(x1, lam, keep(mu), g_ref, depth, cor, terms_second)
    backward(x0, mu, keep_cropped(grad_ref), g_ref, depth, cor, terms_first)


def lat_pack_kernel(margin, reach, own_x, own_c, sea_ref, level_ref, north_msg, south_msg, own_d):
    fields, level_count, rows, cols = own_x.shape
    own_d[...] = (sea_ref[...] * level_ref[...]).astype(jnp.float32)
    planes = fields * level_count
    for f in range(fields):
        for k in range(level_count):
            p = f * level_count + k
            north_msg[margin * p : margin * (p + 1), :] = own_x[f, k, rows - margin : rows, :]
            south_msg[margin * p : margin * (p + 1), :] = own_x[f, k, 0:margin, :]
    north_msg[margin * planes : margin * (planes + 1), :] = own_d[rows - margin : rows, :]
    south_msg[margin * planes : margin * (planes + 1), :] = own_d[0:margin, :]
    base = margin * (planes + 1)
    for f in range(fields):
        for k in range(level_count):
            p = f * level_count + k
            north_msg[base + reach * p : base + reach * (p + 1), :] = own_c[f, k, rows - reach : rows, :]
            south_msg[base + reach * p : base + reach * (p + 1), :] = own_c[f, k, 0:reach, :]


def lon_pack_kernel(margin, reach, own_x, own_c, own_d, north, south, west_msg, east_msg, ext):
    fields, level_count, rows, cols = own_x.shape
    planes = fields * level_count
    frame_rows = ext.shape[0]
    lane = lax.broadcasted_iota(jnp.int32, (frame_rows, 128), 1)
    west_acc = [jnp.zeros((frame_rows, 128), jnp.float32) for _ in range(west_msg.shape[1] // 128)]
    east_acc = [jnp.zeros((frame_rows, 128), jnp.float32) for _ in range(east_msg.shape[1] // 128)]

    def add_plane(p, own, south_rows, north_rows):
        depth = south_rows.shape[0]
        ext[...] = jnp.zeros(ext.shape, jnp.float32)
        ext[0:rows, :] = own
        ext[rows : rows + depth, :] = south_rows
        ext[frame_rows - depth : frame_rows, :] = north_rows
        block, offset = strip_place(p)
        keep = (lane >= offset) & (lane < offset + 12)
        last = shifted(ext[:, cols - 128 : cols], 116 - offset, 1)
        first = shifted(ext[:, 0:128], -offset, 1)
        west_acc[block] = west_acc[block] + jnp.where(keep, last, 0.0)
        east_acc[block] = east_acc[block] + jnp.where(keep, first, 0.0)

    for f in range(fields):
        for k in range(level_count):
            p = f * level_count + k
            add_plane(p, own_x[f, k], south[margin * p : margin * (p + 1), :], north[margin * p : margin * (p + 1), :])
    add_plane(
        planes, own_d[...], south[margin * planes : margin * (planes + 1), :],
        north[margin * planes : margin * (planes + 1), :],
    )
    base = margin * (planes + 1)
    for f in range(fields):
        for k in range(level_count):
            p = f * level_count + k
            add_plane(
                planes + 1 + p, own_c[f, k], south[base + reach * p : base + reach * (p + 1), :],
                north[base + reach * p : base + reach * (p + 1), :],
            )
    for block in range(len(west_acc)):
        west_msg[:, 128 * block : 128 * (block + 1)] = west_acc[block]
        east_msg[:, 128 * block : 128 * (block + 1)] = east_acc[block]


def ring(count, step):
    return [(i, (i + step) % count) for i in range(count)]


def shards(state, cotangent, seamask, levels):
    fields, level_count, row_count, col_count = state.shape
    lat_total = row_count * lax.axis_size("lat")
    lat_start = lax.axis_index("lat") * row_count
    margin = 12
    reach = 6
    rim = 10
    planes = fields * level_count
    vmem = pl.BlockSpec(memory_space=pltpu.VMEM)
    msg_rows = (planes + 1) * rim + planes * reach
    lat_msg = jax.ShapeDtypeStruct((msg_rows, col_count), jnp.float32)
    north_out, south_out, depth = pl.pallas_call(
        functools.partial(lat_pack_kernel, rim, reach),
        out_shape=(lat_msg, lat_msg, jax.ShapeDtypeStruct((row_count, col_count), jnp.float32)),
        in_specs=[vmem] * 4,
        out_specs=(vmem, vmem, vmem),
        interpret=INTERPRET,
    )(state, cotangent, seamask, levels)
    lat_count = lax.axis_size("lat")
    north = lax.ppermute(north_out, "lat", ring(lat_count, 1))
    south = lax.ppermute(south_out, "lat", ring(lat_count, -1))
    frame_rows = row_count + 2 * margin
    frame_cols = -(-(col_count + 2 * margin) // 128) * 128
    msg_cols = 128 * (-(-(2 * planes + 1) // 10))
    lon_msg = jax.ShapeDtypeStruct((frame_rows, msg_cols), jnp.float32)
    west_out, east_out = pl.pallas_call(
        functools.partial(lon_pack_kernel, rim, reach),
        out_shape=(lon_msg, lon_msg),
        in_specs=[vmem] * 5,
        out_specs=(vmem, vmem),
        scratch_shapes=[pltpu.VMEM((frame_rows, col_count), jnp.float32)],
        interpret=INTERPRET,
    )(state, cotangent, depth, north, south)
    lon_count = lax.axis_size("lon")
    west = lax.ppermute(west_out, "lon", ring(lon_count, 1))
    east = lax.ppermute(east_out, "lon", ring(lon_count, -1))
    frame_index = jnp.arange(frame_rows, dtype=jnp.int32)
    global_row = lat_start + jnp.where(frame_index < row_count + margin, frame_index, frame_index - frame_rows)
    rowmask = ((global_row >= 0) & (global_row < lat_total)).astype(jnp.float32)[:, None]
    latitude = jnp.pi * ((global_row.astype(jnp.float32) + 0.5) / lat_total - 0.5)
    cor = (rotation * jnp.sin(latitude))[:, None]
    frame = (fields, level_count, frame_rows, frame_cols)
    out_block = jax.ShapeDtypeStruct((fields, level_count, row_count, col_count), jnp.float32)
    final_state, adjoint_state = pl.pallas_call(
        functools.partial(two_step_kernel, rim, reach),
        out_shape=(out_block, out_block),
        in_specs=[vmem] * 9,
        out_specs=(vmem, vmem),
        scratch_shapes=[pltpu.VMEM(frame, jnp.float32) for _ in range(5)]
        + [pltpu.VMEM((frame_rows, frame_cols), jnp.float32)]
        + [pltpu.VMEM((2,) + frame, jnp.float32) for _ in range(2)],
        interpret=INTERPRET,
    )(state, cotangent, depth, north, south, west, east, rowmask, cor)
    return (final_state, adjoint_state)


def solution(mesh):
    placed = (
        P(None, None, "lat", "lon"),
        P(None, None, "lat", "lon"),
        P("lat", "lon"),
        P("lat", "lon"),
    )
    return jax.shard_map(
        shards,
        mesh=mesh,
        in_specs=placed,
        out_specs=(P(None, None, "lat", "lon"), P(None, None, "lat", "lon")),
        check_vma=False,
    )
```

```python
import jax
import jax.numpy as jnp
from jax import lax
from jax.sharding import PartitionSpec as P
from jax.experimental import pallas as pl
from jax.experimental.pallas import tpu as pltpu
import functools

courant = 0.4
vert_mix = 0.1
rotation = 0.3
buoyancy = 0.3
bottom_drag = 0.2


SIXTIETH = 1.0 / 60.0
INTERPRET = False
CENTRAL = {-2: 1.0, -1: -8.0, 0: 37.0, 1: 37.0, 2: -8.0, 3: 1.0}
DAMPING = {-2: -1.0, -1: 5.0, 0: -10.0, 1: 10.0, 2: -5.0, 3: 1.0}


def shifted(x, step, axis):
    n = x.shape[axis]
    step = step % n
    if step == 0:
        return x
    return pltpu.roll(x, n - step, axis)


def wet_of(depth, k):
    return jnp.where(depth > k + 0.5, 1.0, 0.0)


def bottom_of(depth, k):
    return jnp.where(jnp.abs(depth - (k + 1.0)) < 0.5, 1.0, 0.0)


def face_terms(q, axis):
    m2 = shifted(q, -2, axis)
    m1 = shifted(q, -1, axis)
    p1 = shifted(q, 1, axis)
    p2 = shifted(q, 2, axis)
    p3 = shifted(q, 3, axis)
    central = 37.0 * (q + p1) - 8.0 * (m1 + p2) + (m2 + p3)
    damping = 10.0 * (p1 - q) - 5.0 * (p2 - m1) + (p3 - m2)
    return central, damping


def face_speed(wet, speed, axis):
    open_face = wet * shifted(wet, 1, axis)
    w = 0.5 * (speed + shifted(speed, 1, axis))
    s = jnp.sqrt(w * w + 0.0001)
    return open_face, w, s


def forward(src, store, depth, cor, terms):
    level_count = src.shape[1]
    column = None
    for k in range(level_count):
        wet = wet_of(depth, k)
        bottom = bottom_of(depth, k)
        q = [src[f, k] for f in range(4)]
        density = (-0.2 * q[0] + 0.8 * q[1]) * wet
        column = density if column is None else column + density
        pressure = buoyancy * column
        div = [None] * 4
        for d, (axis, speed) in enumerate(((1, q[2]), (0, q[3]))):
            open_face, w, s = face_speed(wet, speed, axis)
            ratio = w / s
            w = w * SIXTIETH
            s = s * SIXTIETH
            for f in range(4):
                central, damping = face_terms(q[f], axis)
                terms[d, f, k] = central - ratio * damping
                flux = open_face * (w * central - s * damping)
                part = flux - shifted(flux, -1, axis)
                div[f] = part if div[f] is None else div[f] + part
        press_east = 0.5 * (shifted(pressure, 1, 1) - shifted(pressure, -1, 1))
        press_north = 0.5 * (shifted(pressure, 1, 0) - shifted(pressure, -1, 0))
        force = [
            None,
            None,
            cor * q[3] - press_east - bottom_drag * bottom * q[2],
            -cor * q[2] - press_north - bottom_drag * bottom * q[3],
        ]
        for f in range(4):
            vertical = None
            if k > 0:
                vertical = wet_of(depth, k - 1) * (src[f, k - 1] - q[f])
            if k < level_count - 1:
                below = wet_of(depth, k + 1) * (src[f, k + 1] - q[f])
                vertical = below if vertical is None else vertical + below
            value = q[f] - courant * div[f] + vert_mix * vertical
            if force[f] is not None:
                value = value + force[f]
            store(f, k, value * wet)


def backward(x, lam, store, g_ref, depth, cor, terms):
    level_count = x.shape[1]
    for k in range(level_count):
        wet = wet_of(depth, k)
        for f in range(4):
            g_ref[f, k] = wet * lam[f, k]
    density_bar = [None] * level_count
    column = None
    for k in reversed(range(level_count)):
        gu = g_ref[2, k]
        gv = g_ref[3, k]
        pbar = 0.5 * (shifted(gu, 1, 1) - shifted(gu, -1, 1)) + 0.5 * (
            shifted(gv, 1, 0) - shifted(gv, -1, 0)
        )
        column = pbar if column is None else column + pbar
        density_bar[k] = buoyancy * column
    for k in range(level_count):
        wet = wet_of(depth, k)
        bottom = bottom_of(depth, k)
        q = [x[f, k] for f in range(4)]
        g = [g_ref[f, k] for f in range(4)]
        acc = list(g)
        for f in range(4):
            vertical = None
            if k > 0:
                vertical = wet * g_ref[f, k - 1] - wet_of(depth, k - 1) * g[f]
            if k < level_count - 1:
                below = wet * g_ref[f, k + 1] - wet_of(depth, k + 1) * g[f]
                vertical = below if vertical is None else vertical + below
            acc[f] = acc[f] + vert_mix * vertical
        acc[2] = acc[2] - bottom_drag * bottom * g[2] - cor * g[3]
        acc[3] = acc[3] + cor * g[2] - bottom_drag * bottom * g[3]
        acc[0] = acc[0] - 0.2 * wet * density_bar[k]
        acc[1] = acc[1] + 0.8 * wet * density_bar[k]
        div_bar = [-courant * g[f] for f in range(4)]
        for d, (axis, speed_field) in enumerate(((1, 2), (0, 3))):
            open_face, w, s = face_speed(wet, q[speed_field], axis)
            w = w * SIXTIETH
            s = s * SIXTIETH
            w_bar = None
            for f in range(4):
                flux_bar = open_face * (div_bar[f] - shifted(div_bar[f], 1, axis))
                part = flux_bar * terms[d, f, k]
                w_bar = part if w_bar is None else w_bar + part
                alpha = flux_bar * w
                beta = -flux_bar * s
                for j in range(-2, 4):
                    acc[f] = acc[f] + shifted(CENTRAL[j] * alpha + DAMPING[j] * beta, -j, axis)
            acc[speed_field] = acc[speed_field] + (0.5 * SIXTIETH) * (w_bar + shifted(w_bar, -1, axis))
        for f in range(4):
            store(f, k, acc[f])


def strip_place(p):
    return p // 10, 12 * (p % 10)


def assemble(dst, own, south, north, east, west, p, rowmask):
    rows, cols = own.shape
    depth = south.shape[0]
    frame_rows = dst.shape[0]
    dst[...] = jnp.zeros(dst.shape, jnp.float32)
    dst[0:rows, 0:cols] = own
    dst[rows : rows + depth, 0:cols] = south
    dst[frame_rows - depth : frame_rows, 0:cols] = north
    lane = lax.broadcasted_iota(jnp.int32, (frame_rows, 128), 1)
    block, offset = strip_place(p)
    from_east = shifted(east[:, 128 * block : 128 * (block + 1)], offset, 1)
    from_west = shifted(west[:, 128 * block : 128 * (block + 1)], offset - 116, 1)
    dst[:, cols : cols + 128] = jnp.where(lane < 12, from_east, jnp.where(lane >= 116, from_west, 0.0))
    dst[...] = dst[...] * rowmask


def two_step_kernel(
    margin, reach, own_x, own_c, own_d, north, south, west, east, rowmask_ref, cor_ref,
    final_ref, grad_ref, x0, lam, x1, mu, g_ref, depth_ref, terms_first, terms_second,
):
    fields, level_count, rows, cols = own_x.shape
    planes = fields * level_count
    frame_rows = x0.shape[2]
    rowmask = jnp.broadcast_to(rowmask_ref[...], (frame_rows, x0.shape[3]))
    cor = jnp.broadcast_to(cor_ref[...], (frame_rows, x0.shape[3]))
    east_msg = east[...]
    west_msg = west[...]
    for f in range(fields):
        for k in range(level_count):
            p = f * level_count + k
            assemble(
                x0.at[f, k], own_x[f, k], south[margin * p : margin * (p + 1), :],
                north[margin * p : margin * (p + 1), :], east_msg, west_msg, p, rowmask,
            )
    assemble(
        depth_ref, own_d[...], south[margin * planes : margin * (planes + 1), :],
        north[margin * planes : margin * (planes + 1), :], east_msg, west_msg, planes, rowmask,
    )
    base = margin * (planes + 1)
    for f in range(fields):
        for k in range(level_count):
            p = f * level_count + k
            assemble(
                lam.at[f, k], own_c[f, k], south[base + reach * p : base + reach * (p + 1), :],
                north[base + reach * p : base + reach * (p + 1), :], east_msg, west_msg,
                planes + 1 + p, rowmask,
            )
    depth = depth_ref[...]

    def keep(ref):
        def put(f, k, value):
            ref[f, k] = value
        return put

    def keep_cropped(ref):
        def put(f, k, value):
            ref[f, k] = value[:rows, :cols]
        return put

    forward(x0, keep(x1), depth, cor, terms_first)
    forward(x1, keep_cropped(final_ref), depth, cor, terms_second)
    backward(x1, lam, keep(mu), g_ref, depth, cor, terms_second)
    backward(x0, mu, keep_cropped(grad_ref), g_ref, depth, cor, terms_first)


def lat_pack_kernel(margin, reach, own_x, own_c, sea_ref, level_ref, north_msg, south_msg, own_d):
    fields, level_count, rows, cols = own_x.shape
    own_d[...] = (sea_ref[...] * level_ref[...]).astype(jnp.float32)
    planes = fields * level_count
    for f in range(fields):
        for k in range(level_count):
            p = f * level_count + k
            north_msg[margin * p : margin * (p + 1), :] = own_x[f, k, rows - margin : rows, :]
            south_msg[margin * p : margin * (p + 1), :] = own_x[f, k, 0:margin, :]
    north_msg[margin * planes : margin * (planes + 1), :] = own_d[rows - margin : rows, :]
    south_msg[margin * planes : margin * (planes + 1), :] = own_d[0:margin, :]
    base = margin * (planes + 1)
    for f in range(fields):
        for k in range(level_count):
            p = f * level_count + k
            north_msg[base + reach * p : base + reach * (p + 1), :] = own_c[f, k, rows - reach : rows, :]
            south_msg[base + reach * p : base + reach * (p + 1), :] = own_c[f, k, 0:reach, :]


def lon_strips(west_acc, east_acc, lane, p, ext_value):
    cols = ext_value.shape[1]
    block, offset = strip_place(p)
    keep = (lane >= offset) & (lane < offset + 12)
    last = shifted(ext_value[:, cols - 128 : cols], 116 - offset, 1)
    first = shifted(ext_value[:, 0:128], -offset, 1)
    west_acc[block] = west_acc[block] + jnp.where(keep, last, 0.0)
    east_acc[block] = east_acc[block] + jnp.where(keep, first, 0.0)


def lon_pack_own_kernel(own_x, own_c, own_d, west_msg, east_msg):
    fields, level_count, rows, cols = own_x.shape
    planes = fields * level_count
    lane = lax.broadcasted_iota(jnp.int32, (rows, 128), 1)
    blocks = west_msg.shape[1] // 128
    west_acc = [jnp.zeros((rows, 128), jnp.float32) for _ in range(blocks)]
    east_acc = [jnp.zeros((rows, 128), jnp.float32) for _ in range(blocks)]
    for f in range(fields):
        for k in range(level_count):
            p = f * level_count + k
            lon_strips(west_acc, east_acc, lane, p, own_x[f, k])
            lon_strips(west_acc, east_acc, lane, planes + 1 + p, own_c[f, k])
    lon_strips(west_acc, east_acc, lane, planes, own_d[...])
    for block in range(blocks):
        west_msg[:, 128 * block : 128 * (block + 1)] = west_acc[block]
        east_msg[:, 128 * block : 128 * (block + 1)] = east_acc[block]


def lon_pack_halo_kernel(margin, reach, west_own, east_own, north, south, west_msg, east_msg, ext):
    rows = west_own.shape[0]
    planes = (north.shape[0] - margin) // (margin + reach)
    halo_rows = ext.shape[0]
    lane = lax.broadcasted_iota(jnp.int32, (halo_rows, 128), 1)
    blocks = west_msg.shape[1] // 128
    west_acc = [jnp.zeros((halo_rows, 128), jnp.float32) for _ in range(blocks)]
    east_acc = [jnp.zeros((halo_rows, 128), jnp.float32) for _ in range(blocks)]

    def add_plane(p, south_rows, north_rows):
        depth = south_rows.shape[0]
        ext[...] = jnp.zeros(ext.shape, jnp.float32)
        ext[0:depth, :] = south_rows
        ext[halo_rows - depth : halo_rows, :] = north_rows
        lon_strips(west_acc, east_acc, lane, p, ext[...])

    for p in range(planes + 1):
        add_plane(p, south[margin * p : margin * (p + 1), :], north[margin * p : margin * (p + 1), :])
    base = margin * (planes + 1)
    for p in range(planes):
        add_plane(
            planes + 1 + p, south[base + reach * p : base + reach * (p + 1), :],
            north[base + reach * p : base + reach * (p + 1), :],
        )
    west_msg[0:rows, :] = west_own[...]
    east_msg[0:rows, :] = east_own[...]
    for block in range(blocks):
        west_msg[rows:, 128 * block : 128 * (block + 1)] = west_acc[block]
        east_msg[rows:, 128 * block : 128 * (block + 1)] = east_acc[block]


def ring(count, step):
    return [(i, (i + step) % count) for i in range(count)]


def shards(state, cotangent, seamask, levels):
    fields, level_count, row_count, col_count = state.shape
    lat_total = row_count * lax.axis_size("lat")
    lat_start = lax.axis_index("lat") * row_count
    margin = 12
    reach = 6
    rim = 10
    planes = fields * level_count
    vmem = pl.BlockSpec(memory_space=pltpu.VMEM)
    msg_rows = (planes + 1) * rim + planes * reach
    lat_msg = jax.ShapeDtypeStruct((msg_rows, col_count), jnp.float32)
    north_out, south_out, depth = pl.pallas_call(
        functools.partial(lat_pack_kernel, rim, reach),
        out_shape=(lat_msg, lat_msg, jax.ShapeDtypeStruct((row_count, col_count), jnp.float32)),
        in_specs=[vmem] * 4,
        out_specs=(vmem, vmem, vmem),
        interpret=INTERPRET,
    )(state, cotangent, seamask, levels)
    lat_count = lax.axis_size("lat")
    north = lax.ppermute(north_out, "lat", ring(lat_count, 1))
    south = lax.ppermute(south_out, "lat", ring(lat_count, -1))
    frame_rows = row_count + 2 * margin
    frame_cols = -(-(col_count + 2 * margin) // 128) * 128
    msg_cols = 128 * (-(-(2 * planes + 1) // 10))
    lon_msg = jax.ShapeDtypeStruct((frame_rows, msg_cols), jnp.float32)
    own_msg = jax.ShapeDtypeStruct((row_count, msg_cols), jnp.float32)
    west_own, east_own = pl.pallas_call(
        lon_pack_own_kernel,
        out_shape=(own_msg, own_msg),
        in_specs=[vmem] * 3,
        out_specs=(vmem, vmem),
        interpret=INTERPRET,
    )(state, cotangent, depth)
    west_out, east_out = pl.pallas_call(
        functools.partial(lon_pack_halo_kernel, rim, reach),
        out_shape=(lon_msg, lon_msg),
        in_specs=[vmem] * 4,
        out_specs=(vmem, vmem),
        scratch_shapes=[pltpu.VMEM((frame_rows - row_count, col_count), jnp.float32)],
        interpret=INTERPRET,
    )(west_own, east_own, north, south)
    lon_count = lax.axis_size("lon")
    west = lax.ppermute(west_out, "lon", ring(lon_count, 1))
    east = lax.ppermute(east_out, "lon", ring(lon_count, -1))
    frame_index = jnp.arange(frame_rows, dtype=jnp.int32)
    global_row = lat_start + jnp.where(frame_index < row_count + margin, frame_index, frame_index - frame_rows)
    rowmask = ((global_row >= 0) & (global_row < lat_total)).astype(jnp.float32)[:, None]
    latitude = jnp.pi * ((global_row.astype(jnp.float32) + 0.5) / lat_total - 0.5)
    cor = (rotation * jnp.sin(latitude))[:, None]
    frame = (fields, level_count, frame_rows, frame_cols)
    out_block = jax.ShapeDtypeStruct((fields, level_count, row_count, col_count), jnp.float32)
    final_state, adjoint_state = pl.pallas_call(
        functools.partial(two_step_kernel, rim, reach),
        out_shape=(out_block, out_block),
        in_specs=[vmem] * 9,
        out_specs=(vmem, vmem),
        scratch_shapes=[pltpu.VMEM(frame, jnp.float32) for _ in range(5)]
        + [pltpu.VMEM((frame_rows, frame_cols), jnp.float32)]
        + [pltpu.VMEM((2,) + frame, jnp.float32) for _ in range(2)],
        interpret=INTERPRET,
    )(state, cotangent, depth, north, south, west, east, rowmask, cor)
    return (final_state, adjoint_state)


def solution(mesh):
    placed = (
        P(None, None, "lat", "lon"),
        P(None, None, "lat", "lon"),
        P("lat", "lon"),
        P("lat", "lon"),
    )
    return jax.shard_map(
        shards,
        mesh=mesh,
        in_specs=placed,
        out_specs=(P(None, None, "lat", "lon"), P(None, None, "lat", "lon")),
        check_vma=False,
    )
```

```python
import jax
import jax.numpy as jnp
from jax import lax
from jax.sharding import PartitionSpec as P
from jax.experimental import pallas as pl
from jax.experimental.pallas import tpu as pltpu
import functools

courant = 0.4
vert_mix = 0.1
rotation = 0.3
buoyancy = 0.3
bottom_drag = 0.2


SIXTIETH = 1.0 / 60.0
INTERPRET = False
CENTRAL = {-2: 1.0, -1: -8.0, 0: 37.0, 1: 37.0, 2: -8.0, 3: 1.0}
DAMPING = {-2: -1.0, -1: 5.0, 0: -10.0, 1: 10.0, 2: -5.0, 3: 1.0}


def shifted(x, step, axis):
    n = x.shape[axis]
    step = step % n
    if step == 0:
        return x
    return pltpu.roll(x, n - step, axis)


def wet_of(depth, k):
    return jnp.where(depth > k + 0.5, 1.0, 0.0)


def bottom_of(depth, k):
    return jnp.where(jnp.abs(depth - (k + 1.0)) < 0.5, 1.0, 0.0)


def face_terms(q, axis):
    m2 = shifted(q, -2, axis)
    m1 = shifted(q, -1, axis)
    p1 = shifted(q, 1, axis)
    p2 = shifted(q, 2, axis)
    p3 = shifted(q, 3, axis)
    central = 37.0 * (q + p1) - 8.0 * (m1 + p2) + (m2 + p3)
    damping = 10.0 * (p1 - q) - 5.0 * (p2 - m1) + (p3 - m2)
    return central, damping


def face_speed(wet, speed, axis):
    open_face = wet * shifted(wet, 1, axis)
    w = 0.5 * (speed + shifted(speed, 1, axis))
    s = jnp.sqrt(w * w + 0.0001)
    return open_face, w, s


def forward(src, store, depth, cor, terms, faces):
    level_count = src.shape[1]
    column = None
    for k in range(level_count):
        wet = wet_of(depth, k)
        bottom = bottom_of(depth, k)
        q = [src[f, k] for f in range(4)]
        density = (-0.2 * q[0] + 0.8 * q[1]) * wet
        column = density if column is None else column + density
        pressure = buoyancy * column
        div = [None] * 4
        for d, (axis, speed) in enumerate(((1, q[2]), (0, q[3]))):
            open_face, w, s = face_speed(wet, speed, axis)
            ratio = w / s
            w = w * SIXTIETH
            s = s * SIXTIETH
            faces[d, k, 0] = open_face
            faces[d, k, 1] = w
            faces[d, k, 2] = s
            for f in range(4):
                central, damping = face_terms(q[f], axis)
                terms[d, f, k] = central - ratio * damping
                flux = open_face * (w * central - s * damping)
                part = flux - shifted(flux, -1, axis)
                div[f] = part if div[f] is None else div[f] + part
        press_east = 0.5 * (shifted(pressure, 1, 1) - shifted(pressure, -1, 1))
        press_north = 0.5 * (shifted(pressure, 1, 0) - shifted(pressure, -1, 0))
        force = [
            None,
            None,
            cor * q[3] - press_east - bottom_drag * bottom * q[2],
            -cor * q[2] - press_north - bottom_drag * bottom * q[3],
        ]
        for f in range(4):
            vertical = None
            if k > 0:
                vertical = wet_of(depth, k - 1) * (src[f, k - 1] - q[f])
            if k < level_count - 1:
                below = wet_of(depth, k + 1) * (src[f, k + 1] - q[f])
                vertical = below if vertical is None else vertical + below
            value = q[f] - courant * div[f] + vert_mix * vertical
            if force[f] is not None:
                value = value + force[f]
            store(f, k, value * wet)


def backward(x, lam, store, g_ref, depth, cor, terms, faces):
    level_count = x.shape[1]
    for k in range(level_count):
        wet = wet_of(depth, k)
        for f in range(4):
            g_ref[f, k] = wet * lam[f, k]
    density_bar = [None] * level_count
    column = None
    for k in reversed(range(level_count)):
        gu = g_ref[2, k]
        gv = g_ref[3, k]
        pbar = 0.5 * (shifted(gu, 1, 1) - shifted(gu, -1, 1)) + 0.5 * (
            shifted(gv, 1, 0) - shifted(gv, -1, 0)
        )
        column = pbar if column is None else column + pbar
        density_bar[k] = buoyancy * column
    for k in range(level_count):
        wet = wet_of(depth, k)
        bottom = bottom_of(depth, k)
        q = [x[f, k] for f in range(4)]
        g = [g_ref[f, k] for f in range(4)]
        acc = list(g)
        for f in range(4):
            vertical = None
            if k > 0:
                vertical = wet * g_ref[f, k - 1] - wet_of(depth, k - 1) * g[f]
            if k < level_count - 1:
                below = wet * g_ref[f, k + 1] - wet_of(depth, k + 1) * g[f]
                vertical = below if vertical is None else vertical + below
            acc[f] = acc[f] + vert_mix * vertical
        acc[2] = acc[2] - bottom_drag * bottom * g[2] - cor * g[3]
        acc[3] = acc[3] + cor * g[2] - bottom_drag * bottom * g[3]
        acc[0] = acc[0] - 0.2 * wet * density_bar[k]
        acc[1] = acc[1] + 0.8 * wet * density_bar[k]
        div_bar = [-courant * g[f] for f in range(4)]
        for d, (axis, speed_field) in enumerate(((1, 2), (0, 3))):
            open_face = faces[d, k, 0]
            w = faces[d, k, 1]
            s = faces[d, k, 2]
            w_bar = None
            for f in range(4):
                flux_bar = open_face * (div_bar[f] - shifted(div_bar[f], 1, axis))
                part = flux_bar * terms[d, f, k]
                w_bar = part if w_bar is None else w_bar + part
                alpha = flux_bar * w
                beta = -flux_bar * s
                for j in range(-2, 4):
                    acc[f] = acc[f] + shifted(CENTRAL[j] * alpha + DAMPING[j] * beta, -j, axis)
            acc[speed_field] = acc[speed_field] + (0.5 * SIXTIETH) * (w_bar + shifted(w_bar, -1, axis))
        for f in range(4):
            store(f, k, acc[f])


def strip_place(p):
    return p // 10, 12 * (p % 10)


def assemble(dst, own, south, north, east, west, p, rowmask):
    rows, cols = own.shape
    depth = south.shape[0]
    frame_rows = dst.shape[0]
    dst[...] = jnp.zeros(dst.shape, jnp.float32)
    dst[0:rows, 0:cols] = own
    dst[rows : rows + depth, 0:cols] = south
    dst[frame_rows - depth : frame_rows, 0:cols] = north
    lane = lax.broadcasted_iota(jnp.int32, (frame_rows, 128), 1)
    block, offset = strip_place(p)
    from_east = shifted(east[:, 128 * block : 128 * (block + 1)], offset, 1)
    from_west = shifted(west[:, 128 * block : 128 * (block + 1)], offset - 116, 1)
    dst[:, cols : cols + 128] = jnp.where(lane < 12, from_east, jnp.where(lane >= 116, from_west, 0.0))
    dst[...] = dst[...] * rowmask


def two_step_kernel(
    margin, reach, own_x, own_c, own_d, north, south, west, east, rowmask_ref, cor_ref,
    final_ref, grad_ref, x0, lam, x1, mu, g_ref, depth_ref, terms_first, terms_second,
    faces_first, faces_second,
):
    fields, level_count, rows, cols = own_x.shape
    planes = fields * level_count
    frame_rows = x0.shape[2]
    rowmask = jnp.broadcast_to(rowmask_ref[...], (frame_rows, x0.shape[3]))
    cor = jnp.broadcast_to(cor_ref[...], (frame_rows, x0.shape[3]))
    east_msg = east[...]
    west_msg = west[...]
    for f in range(fields):
        for k in range(level_count):
            p = f * level_count + k
            assemble(
                x0.at[f, k], own_x[f, k], south[margin * p : margin * (p + 1), :],
                north[margin * p : margin * (p + 1), :], east_msg, west_msg, p, rowmask,
            )
    assemble(
        depth_ref, own_d[...], south[margin * planes : margin * (planes + 1), :],
        north[margin * planes : margin * (planes + 1), :], east_msg, west_msg, planes, rowmask,
    )
    base = margin * (planes + 1)
    for f in range(fields):
        for k in range(level_count):
            p = f * level_count + k
            assemble(
                lam.at[f, k], own_c[f, k], south[base + reach * p : base + reach * (p + 1), :],
                north[base + reach * p : base + reach * (p + 1), :], east_msg, west_msg,
                planes + 1 + p, rowmask,
            )
    depth = depth_ref[...]

    def keep(ref):
        def put(f, k, value):
            ref[f, k] = value
        return put

    def keep_cropped(ref):
        def put(f, k, value):
            ref[f, k] = value[:rows, :cols]
        return put

    forward(x0, keep(x1), depth, cor, terms_first, faces_first)
    forward(x1, keep_cropped(final_ref), depth, cor, terms_second, faces_second)
    backward(x1, lam, keep(mu), g_ref, depth, cor, terms_second, faces_second)
    backward(x0, mu, keep_cropped(grad_ref), g_ref, depth, cor, terms_first, faces_first)


def lat_pack_kernel(margin, reach, own_x, own_c, sea_ref, level_ref, north_msg, south_msg, own_d):
    fields, level_count, rows, cols = own_x.shape
    own_d[...] = (sea_ref[...] * level_ref[...]).astype(jnp.float32)
    planes = fields * level_count
    for f in range(fields):
        for k in range(level_count):
            p = f * level_count + k
            north_msg[margin * p : margin * (p + 1), :] = own_x[f, k, rows - margin : rows, :]
            south_msg[margin * p : margin * (p + 1), :] = own_x[f, k, 0:margin, :]
    north_msg[margin * planes : margin * (planes + 1), :] = own_d[rows - margin : rows, :]
    south_msg[margin * planes : margin * (planes + 1), :] = own_d[0:margin, :]
    base = margin * (planes + 1)
    for f in range(fields):
        for k in range(level_count):
            p = f * level_count + k
            north_msg[base + reach * p : base + reach * (p + 1), :] = own_c[f, k, rows - reach : rows, :]
            south_msg[base + reach * p : base + reach * (p + 1), :] = own_c[f, k, 0:reach, :]


def lon_strips(west_acc, east_acc, lane, p, ext_value):
    cols = ext_value.shape[1]
    block, offset = strip_place(p)
    keep = (lane >= offset) & (lane < offset + 12)
    last = shifted(ext_value[:, cols - 128 : cols], 116 - offset, 1)
    first = shifted(ext_value[:, 0:128], -offset, 1)
    west_acc[block] = west_acc[block] + jnp.where(keep, last, 0.0)
    east_acc[block] = east_acc[block] + jnp.where(keep, first, 0.0)


def lon_pack_own_kernel(own_x, own_c, own_d, west_msg, east_msg):
    fields, level_count, rows, cols = own_x.shape
    planes = fields * level_count
    lane = lax.broadcasted_iota(jnp.int32, (rows, 128), 1)
    blocks = west_msg.shape[1] // 128
    west_acc = [jnp.zeros((rows, 128), jnp.float32) for _ in range(blocks)]
    east_acc = [jnp.zeros((rows, 128), jnp.float32) for _ in range(blocks)]
    for f in range(fields):
        for k in range(level_count):
            p = f * level_count + k
            lon_strips(west_acc, east_acc, lane, p, own_x[f, k])
            lon_strips(west_acc, east_acc, lane, planes + 1 + p, own_c[f, k])
    lon_strips(west_acc, east_acc, lane, planes, own_d[...])
    for block in range(blocks):
        west_msg[:, 128 * block : 128 * (block + 1)] = west_acc[block]
        east_msg[:, 128 * block : 128 * (block + 1)] = east_acc[block]


def lon_pack_halo_kernel(margin, reach, west_own, east_own, north, south, west_msg, east_msg, ext):
    rows = west_own.shape[0]
    planes = (north.shape[0] - margin) // (margin + reach)
    halo_rows = ext.shape[0]
    lane = lax.broadcasted_iota(jnp.int32, (halo_rows, 128), 1)
    blocks = west_msg.shape[1] // 128
    west_acc = [jnp.zeros((halo_rows, 128), jnp.float32) for _ in range(blocks)]
    east_acc = [jnp.zeros((halo_rows, 128), jnp.float32) for _ in range(blocks)]

    def add_plane(p, south_rows, north_rows):
        depth = south_rows.shape[0]
        ext[...] = jnp.zeros(ext.shape, jnp.float32)
        ext[0:depth, :] = south_rows
        ext[halo_rows - depth : halo_rows, :] = north_rows
        lon_strips(west_acc, east_acc, lane, p, ext[...])

    for p in range(planes + 1):
        add_plane(p, south[margin * p : margin * (p + 1), :], north[margin * p : margin * (p + 1), :])
    base = margin * (planes + 1)
    for p in range(planes):
        add_plane(
            planes + 1 + p, south[base + reach * p : base + reach * (p + 1), :],
            north[base + reach * p : base + reach * (p + 1), :],
        )
    west_msg[0:rows, :] = west_own[...]
    east_msg[0:rows, :] = east_own[...]
    for block in range(blocks):
        west_msg[rows:, 128 * block : 128 * (block + 1)] = west_acc[block]
        east_msg[rows:, 128 * block : 128 * (block + 1)] = east_acc[block]


def ring(count, step):
    return [(i, (i + step) % count) for i in range(count)]


def shards(state, cotangent, seamask, levels):
    fields, level_count, row_count, col_count = state.shape
    lat_total = row_count * lax.axis_size("lat")
    lat_start = lax.axis_index("lat") * row_count
    margin = 12
    reach = 6
    rim = 10
    planes = fields * level_count
    vmem = pl.BlockSpec(memory_space=pltpu.VMEM)
    msg_rows = (planes + 1) * rim + planes * reach
    lat_msg = jax.ShapeDtypeStruct((msg_rows, col_count), jnp.float32)
    north_out, south_out, depth = pl.pallas_call(
        functools.partial(lat_pack_kernel, rim, reach),
        out_shape=(lat_msg, lat_msg, jax.ShapeDtypeStruct((row_count, col_count), jnp.float32)),
        in_specs=[vmem] * 4,
        out_specs=(vmem, vmem, vmem),
        interpret=INTERPRET,
    )(state, cotangent, seamask, levels)
    lat_count = lax.axis_size("lat")
    north = lax.ppermute(north_out, "lat", ring(lat_count, 1))
    south = lax.ppermute(south_out, "lat", ring(lat_count, -1))
    frame_rows = row_count + 2 * margin
    frame_cols = -(-(col_count + 2 * margin) // 128) * 128
    msg_cols = 128 * (-(-(2 * planes + 1) // 10))
    lon_msg = jax.ShapeDtypeStruct((frame_rows, msg_cols), jnp.float32)
    own_msg = jax.ShapeDtypeStruct((row_count, msg_cols), jnp.float32)
    west_own, east_own = pl.pallas_call(
        lon_pack_own_kernel,
        out_shape=(own_msg, own_msg),
        in_specs=[vmem] * 3,
        out_specs=(vmem, vmem),
        interpret=INTERPRET,
    )(state, cotangent, depth)
    west_out, east_out = pl.pallas_call(
        functools.partial(lon_pack_halo_kernel, rim, reach),
        out_shape=(lon_msg, lon_msg),
        in_specs=[vmem] * 4,
        out_specs=(vmem, vmem),
        scratch_shapes=[pltpu.VMEM((frame_rows - row_count, col_count), jnp.float32)],
        interpret=INTERPRET,
    )(west_own, east_own, north, south)
    lon_count = lax.axis_size("lon")
    west = lax.ppermute(west_out, "lon", ring(lon_count, 1))
    east = lax.ppermute(east_out, "lon", ring(lon_count, -1))
    frame_index = jnp.arange(frame_rows, dtype=jnp.int32)
    global_row = lat_start + jnp.where(frame_index < row_count + margin, frame_index, frame_index - frame_rows)
    rowmask = ((global_row >= 0) & (global_row < lat_total)).astype(jnp.float32)[:, None]
    latitude = jnp.pi * ((global_row.astype(jnp.float32) + 0.5) / lat_total - 0.5)
    cor = (rotation * jnp.sin(latitude))[:, None]
    frame = (fields, level_count, frame_rows, frame_cols)
    out_block = jax.ShapeDtypeStruct((fields, level_count, row_count, col_count), jnp.float32)
    final_state, adjoint_state = pl.pallas_call(
        functools.partial(two_step_kernel, rim, reach),
        out_shape=(out_block, out_block),
        in_specs=[vmem] * 9,
        out_specs=(vmem, vmem),
        scratch_shapes=[pltpu.VMEM(frame, jnp.float32) for _ in range(5)]
        + [pltpu.VMEM((frame_rows, frame_cols), jnp.float32)]
        + [pltpu.VMEM((2,) + frame, jnp.float32) for _ in range(2)]
        + [pltpu.VMEM((2, level_count, 3, frame_rows, frame_cols), jnp.float32) for _ in range(2)],
        interpret=INTERPRET,
    )(state, cotangent, depth, north, south, west, east, rowmask, cor)
    return (final_state, adjoint_state)


def solution(mesh):
    placed = (
        P(None, None, "lat", "lon"),
        P(None, None, "lat", "lon"),
        P("lat", "lon"),
        P("lat", "lon"),
    )
    return jax.shard_map(
        shards,
        mesh=mesh,
        in_specs=placed,
        out_specs=(P(None, None, "lat", "lon"), P(None, None, "lat", "lon")),
        check_vma=False,
    )
```

```python
import jax
import jax.numpy as jnp
from jax import lax
from jax.sharding import PartitionSpec as P
from jax.experimental import pallas as pl
from jax.experimental.pallas import tpu as pltpu
import functools

courant = 0.4
vert_mix = 0.1
rotation = 0.3
buoyancy = 0.3
bottom_drag = 0.2


SIXTIETH = 1.0 / 60.0
INTERPRET = False
CENTRAL = {-2: 1.0, -1: -8.0, 0: 37.0, 1: 37.0, 2: -8.0, 3: 1.0}
DAMPING = {-2: -1.0, -1: 5.0, 0: -10.0, 1: 10.0, 2: -5.0, 3: 1.0}


def shifted(x, step, axis):
    n = x.shape[axis]
    step = step % n
    if step == 0:
        return x
    return pltpu.roll(x, n - step, axis)


def wet_of(depth, k):
    return jnp.where(depth > k + 0.5, 1.0, 0.0)


def bottom_of(depth, k):
    return jnp.where(jnp.abs(depth - (k + 1.0)) < 0.5, 1.0, 0.0)


def face_terms(q, axis):
    m2 = shifted(q, -2, axis)
    m1 = shifted(q, -1, axis)
    p1 = shifted(q, 1, axis)
    p2 = shifted(q, 2, axis)
    p3 = shifted(q, 3, axis)
    central = 37.0 * (q + p1) - 8.0 * (m1 + p2) + (m2 + p3)
    damping = 10.0 * (p1 - q) - 5.0 * (p2 - m1) + (p3 - m2)
    return central, damping


def face_speed(wet, speed, axis):
    open_face = wet * shifted(wet, 1, axis)
    w = 0.5 * (speed + shifted(speed, 1, axis))
    s = jnp.sqrt(w * w + 0.0001)
    return open_face, w, s


def forward(src, store, depth, cor, terms, faces):
    level_count = src.shape[1]
    column = None
    for k in range(level_count):
        wet = wet_of(depth, k)
        bottom = bottom_of(depth, k)
        q = [src[f, k] for f in range(4)]
        density = (-0.2 * q[0] + 0.8 * q[1]) * wet
        column = density if column is None else column + density
        pressure = buoyancy * column
        div = [None] * 4
        for d, (axis, speed) in enumerate(((1, q[2]), (0, q[3]))):
            open_face, w, s = face_speed(wet, speed, axis)
            ratio = w / s
            w = w * SIXTIETH
            s = s * SIXTIETH
            faces[d, k, 0] = open_face
            faces[d, k, 1] = w
            faces[d, k, 2] = s
            for f in range(4):
                central, damping = face_terms(q[f], axis)
                terms[d, f, k] = central - ratio * damping
                flux = open_face * (w * central - s * damping)
                part = flux - shifted(flux, -1, axis)
                div[f] = part if div[f] is None else div[f] + part
        press_east = 0.5 * (shifted(pressure, 1, 1) - shifted(pressure, -1, 1))
        press_north = 0.5 * (shifted(pressure, 1, 0) - shifted(pressure, -1, 0))
        force = [
            None,
            None,
            cor * q[3] - press_east - bottom_drag * bottom * q[2],
            -cor * q[2] - press_north - bottom_drag * bottom * q[3],
        ]
        for f in range(4):
            vertical = None
            if k > 0:
                vertical = wet_of(depth, k - 1) * (src[f, k - 1] - q[f])
            if k < level_count - 1:
                below = wet_of(depth, k + 1) * (src[f, k + 1] - q[f])
                vertical = below if vertical is None else vertical + below
            value = q[f] - courant * div[f] + vert_mix * vertical
            if force[f] is not None:
                value = value + force[f]
            store(f, k, value * wet)


def backward(x, lam, store, g_ref, depth, cor, terms, faces):
    level_count = x.shape[1]
    for k in range(level_count):
        wet = wet_of(depth, k)
        for f in range(4):
            g_ref[f, k] = wet * lam[f, k]
    density_bar = [None] * level_count
    column = None
    for k in reversed(range(level_count)):
        gu = g_ref[2, k]
        gv = g_ref[3, k]
        pbar = 0.5 * (shifted(gu, 1, 1) - shifted(gu, -1, 1)) + 0.5 * (
            shifted(gv, 1, 0) - shifted(gv, -1, 0)
        )
        column = pbar if column is None else column + pbar
        density_bar[k] = buoyancy * column
    for k in range(level_count):
        wet = wet_of(depth, k)
        bottom = bottom_of(depth, k)
        q = [x[f, k] for f in range(4)]
        g = [g_ref[f, k] for f in range(4)]
        acc = list(g)
        for f in range(4):
            vertical = None
            if k > 0:
                vertical = wet * g_ref[f, k - 1] - wet_of(depth, k - 1) * g[f]
            if k < level_count - 1:
                below = wet * g_ref[f, k + 1] - wet_of(depth, k + 1) * g[f]
                vertical = below if vertical is None else vertical + below
            acc[f] = acc[f] + vert_mix * vertical
        acc[2] = acc[2] - bottom_drag * bottom * g[2] - cor * g[3]
        acc[3] = acc[3] + cor * g[2] - bottom_drag * bottom * g[3]
        acc[0] = acc[0] - 0.2 * wet * density_bar[k]
        acc[1] = acc[1] + 0.8 * wet * density_bar[k]
        div_bar = [-courant * g[f] for f in range(4)]
        for d, (axis, speed_field) in enumerate(((1, 2), (0, 3))):
            open_face = faces[d, k, 0]
            w = faces[d, k, 1]
            s = faces[d, k, 2]
            w_bar = None
            for f in range(4):
                flux_bar = open_face * (div_bar[f] - shifted(div_bar[f], 1, axis))
                part = flux_bar * terms[d, f, k]
                w_bar = part if w_bar is None else w_bar + part
                alpha = flux_bar * w
                beta = -flux_bar * s
                alpha8 = 8.0 * alpha
                beta5 = 5.0 * beta
                alpha37 = 37.0 * alpha
                beta10 = 10.0 * beta
                acc[f] = (
                    acc[f]
                    + (alpha37 - beta10)
                    + shifted(alpha - beta, 2, axis)
                    + shifted(beta5 - alpha8, 1, axis)
                    + shifted(alpha37 + beta10, -1, axis)
                    - shifted(alpha8 + beta5, -2, axis)
                    + shifted(alpha + beta, -3, axis)
                )
            acc[speed_field] = acc[speed_field] + (0.5 * SIXTIETH) * (w_bar + shifted(w_bar, -1, axis))
        for f in range(4):
            store(f, k, acc[f])


def strip_place(p):
    return p // 10, 12 * (p % 10)


def assemble(dst, own, south, north, east, west, p, rowmask):
    rows, cols = own.shape
    depth = south.shape[0]
    frame_rows = dst.shape[0]
    dst[...] = jnp.zeros(dst.shape, jnp.float32)
    dst[0:rows, 0:cols] = own
    dst[rows : rows + depth, 0:cols] = south
    dst[frame_rows - depth : frame_rows, 0:cols] = north
    lane = lax.broadcasted_iota(jnp.int32, (frame_rows, 128), 1)
    block, offset = strip_place(p)
    from_east = shifted(east[:, 128 * block : 128 * (block + 1)], offset, 1)
    from_west = shifted(west[:, 128 * block : 128 * (block + 1)], offset - 116, 1)
    dst[:, cols : cols + 128] = jnp.where(lane < 12, from_east, jnp.where(lane >= 116, from_west, 0.0))
    dst[...] = dst[...] * rowmask


def two_step_kernel(
    margin, reach, own_x, own_c, own_d, north, south, west, east, rowmask_ref, cor_ref,
    final_ref, grad_ref, x0, lam, x1, mu, g_ref, depth_ref, terms_first, terms_second,
    faces_first, faces_second,
):
    fields, level_count, rows, cols = own_x.shape
    planes = fields * level_count
    frame_rows = x0.shape[2]
    rowmask = jnp.broadcast_to(rowmask_ref[...], (frame_rows, x0.shape[3]))
    cor = jnp.broadcast_to(cor_ref[...], (frame_rows, x0.shape[3]))
    east_msg = east[...]
    west_msg = west[...]
    for f in range(fields):
        for k in range(level_count):
            p = f * level_count + k
            assemble(
                x0.at[f, k], own_x[f, k], south[margin * p : margin * (p + 1), :],
                north[margin * p : margin * (p + 1), :], east_msg, west_msg, p, rowmask,
            )
    assemble(
        depth_ref, own_d[...], south[margin * planes : margin * (planes + 1), :],
        north[margin * planes : margin * (planes + 1), :], east_msg, west_msg, planes, rowmask,
    )
    base = margin * (planes + 1)
    for f in range(fields):
        for k in range(level_count):
            p = f * level_count + k
            assemble(
                lam.at[f, k], own_c[f, k], south[base + reach * p : base + reach * (p + 1), :],
                north[base + reach * p : base + reach * (p + 1), :], east_msg, west_msg,
                planes + 1 + p, rowmask,
            )
    depth = depth_ref[...]

    def keep(ref):
        def put(f, k, value):
            ref[f, k] = value
        return put

    def keep_cropped(ref):
        def put(f, k, value):
            ref[f, k] = value[:rows, :cols]
        return put

    forward(x0, keep(x1), depth, cor, terms_first, faces_first)
    forward(x1, keep_cropped(final_ref), depth, cor, terms_second, faces_second)
    backward(x1, lam, keep(mu), g_ref, depth, cor, terms_second, faces_second)
    backward(x0, mu, keep_cropped(grad_ref), g_ref, depth, cor, terms_first, faces_first)


def lat_pack_kernel(margin, reach, own_x, own_c, sea_ref, level_ref, north_msg, south_msg, own_d):
    fields, level_count, rows, cols = own_x.shape
    own_d[...] = (sea_ref[...] * level_ref[...]).astype(jnp.float32)
    planes = fields * level_count
    for f in range(fields):
        for k in range(level_count):
            p = f * level_count + k
            north_msg[margin * p : margin * (p + 1), :] = own_x[f, k, rows - margin : rows, :]
            south_msg[margin * p : margin * (p + 1), :] = own_x[f, k, 0:margin, :]
    north_msg[margin * planes : margin * (planes + 1), :] = own_d[rows - margin : rows, :]
    south_msg[margin * planes : margin * (planes + 1), :] = own_d[0:margin, :]
    base = margin * (planes + 1)
    for f in range(fields):
        for k in range(level_count):
            p = f * level_count + k
            north_msg[base + reach * p : base + reach * (p + 1), :] = own_c[f, k, rows - reach : rows, :]
            south_msg[base + reach * p : base + reach * (p + 1), :] = own_c[f, k, 0:reach, :]


def lon_strips(west_acc, east_acc, lane, p, ext_value):
    cols = ext_value.shape[1]
    block, offset = strip_place(p)
    keep = (lane >= offset) & (lane < offset + 12)
    last = shifted(ext_value[:, cols - 128 : cols], 116 - offset, 1)
    first = shifted(ext_value[:, 0:128], -offset, 1)
    west_acc[block] = west_acc[block] + jnp.where(keep, last, 0.0)
    east_acc[block] = east_acc[block] + jnp.where(keep, first, 0.0)


def lon_pack_own_kernel(own_x, own_c, own_d, west_msg, east_msg):
    fields, level_count, rows, cols = own_x.shape
    planes = fields * level_count
    lane = lax.broadcasted_iota(jnp.int32, (rows, 128), 1)
    blocks = west_msg.shape[1] // 128
    west_acc = [jnp.zeros((rows, 128), jnp.float32) for _ in range(blocks)]
    east_acc = [jnp.zeros((rows, 128), jnp.float32) for _ in range(blocks)]
    for f in range(fields):
        for k in range(level_count):
            p = f * level_count + k
            lon_strips(west_acc, east_acc, lane, p, own_x[f, k])
            lon_strips(west_acc, east_acc, lane, planes + 1 + p, own_c[f, k])
    lon_strips(west_acc, east_acc, lane, planes, own_d[...])
    for block in range(blocks):
        west_msg[:, 128 * block : 128 * (block + 1)] = west_acc[block]
        east_msg[:, 128 * block : 128 * (block + 1)] = east_acc[block]


def lon_pack_halo_kernel(margin, reach, west_own, east_own, north, south, west_msg, east_msg, ext):
    rows = west_own.shape[0]
    planes = (north.shape[0] - margin) // (margin + reach)
    halo_rows = ext.shape[0]
    lane = lax.broadcasted_iota(jnp.int32, (halo_rows, 128), 1)
    blocks = west_msg.shape[1] // 128
    west_acc = [jnp.zeros((halo_rows, 128), jnp.float32) for _ in range(blocks)]
    east_acc = [jnp.zeros((halo_rows, 128), jnp.float32) for _ in range(blocks)]

    def add_plane(p, south_rows, north_rows):
        depth = south_rows.shape[0]
        ext[...] = jnp.zeros(ext.shape, jnp.float32)
        ext[0:depth, :] = south_rows
        ext[halo_rows - depth : halo_rows, :] = north_rows
        lon_strips(west_acc, east_acc, lane, p, ext[...])

    for p in range(planes + 1):
        add_plane(p, south[margin * p : margin * (p + 1), :], north[margin * p : margin * (p + 1), :])
    base = margin * (planes + 1)
    for p in range(planes):
        add_plane(
            planes + 1 + p, south[base + reach * p : base + reach * (p + 1), :],
            north[base + reach * p : base + reach * (p + 1), :],
        )
    west_msg[0:rows, :] = west_own[...]
    east_msg[0:rows, :] = east_own[...]
    for block in range(blocks):
        west_msg[rows:, 128 * block : 128 * (block + 1)] = west_acc[block]
        east_msg[rows:, 128 * block : 128 * (block + 1)] = east_acc[block]


def ring(count, step):
    return [(i, (i + step) % count) for i in range(count)]


def shards(state, cotangent, seamask, levels):
    fields, level_count, row_count, col_count = state.shape
    lat_total = row_count * lax.axis_size("lat")
    lat_start = lax.axis_index("lat") * row_count
    margin = 12
    reach = 6
    rim = 10
    planes = fields * level_count
    vmem = pl.BlockSpec(memory_space=pltpu.VMEM)
    msg_rows = (planes + 1) * rim + planes * reach
    lat_msg = jax.ShapeDtypeStruct((msg_rows, col_count), jnp.float32)
    north_out, south_out, depth = pl.pallas_call(
        functools.partial(lat_pack_kernel, rim, reach),
        out_shape=(lat_msg, lat_msg, jax.ShapeDtypeStruct((row_count, col_count), jnp.float32)),
        in_specs=[vmem] * 4,
        out_specs=(vmem, vmem, vmem),
        interpret=INTERPRET,
    )(state, cotangent, seamask, levels)
    lat_count = lax.axis_size("lat")
    north = lax.ppermute(north_out, "lat", ring(lat_count, 1))
    south = lax.ppermute(south_out, "lat", ring(lat_count, -1))
    frame_rows = row_count + 2 * margin
    frame_cols = -(-(col_count + 2 * margin) // 128) * 128
    msg_cols = 128 * (-(-(2 * planes + 1) // 10))
    lon_msg = jax.ShapeDtypeStruct((frame_rows, msg_cols), jnp.float32)
    own_msg = jax.ShapeDtypeStruct((row_count, msg_cols), jnp.float32)
    west_own, east_own = pl.pallas_call(
        lon_pack_own_kernel,
        out_shape=(own_msg, own_msg),
        in_specs=[vmem] * 3,
        out_specs=(vmem, vmem),
        interpret=INTERPRET,
    )(state, cotangent, depth)
    west_out, east_out = pl.pallas_call(
        functools.partial(lon_pack_halo_kernel, rim, reach),
        out_shape=(lon_msg, lon_msg),
        in_specs=[vmem] * 4,
        out_specs=(vmem, vmem),
        scratch_shapes=[pltpu.VMEM((frame_rows - row_count, col_count), jnp.float32)],
        interpret=INTERPRET,
    )(west_own, east_own, north, south)
    lon_count = lax.axis_size("lon")
    west = lax.ppermute(west_out, "lon", ring(lon_count, 1))
    east = lax.ppermute(east_out, "lon", ring(lon_count, -1))
    frame_index = jnp.arange(frame_rows, dtype=jnp.int32)
    global_row = lat_start + jnp.where(frame_index < row_count + margin, frame_index, frame_index - frame_rows)
    rowmask = ((global_row >= 0) & (global_row < lat_total)).astype(jnp.float32)[:, None]
    latitude = jnp.pi * ((global_row.astype(jnp.float32) + 0.5) / lat_total - 0.5)
    cor = (rotation * jnp.sin(latitude))[:, None]
    frame = (fields, level_count, frame_rows, frame_cols)
    out_block = jax.ShapeDtypeStruct((fields, level_count, row_count, col_count), jnp.float32)
    final_state, adjoint_state = pl.pallas_call(
        functools.partial(two_step_kernel, rim, reach),
        out_shape=(out_block, out_block),
        in_specs=[vmem] * 9,
        out_specs=(vmem, vmem),
        scratch_shapes=[pltpu.VMEM(frame, jnp.float32) for _ in range(5)]
        + [pltpu.VMEM((frame_rows, frame_cols), jnp.float32)]
        + [pltpu.VMEM((2,) + frame, jnp.float32) for _ in range(2)]
        + [pltpu.VMEM((2, level_count, 3, frame_rows, frame_cols), jnp.float32) for _ in range(2)],
        interpret=INTERPRET,
    )(state, cotangent, depth, north, south, west, east, rowmask, cor)
    return (final_state, adjoint_state)


def solution(mesh):
    placed = (
        P(None, None, "lat", "lon"),
        P(None, None, "lat", "lon"),
        P("lat", "lon"),
        P("lat", "lon"),
    )
    return jax.shard_map(
        shards,
        mesh=mesh,
        in_specs=placed,
        out_specs=(P(None, None, "lat", "lon"), P(None, None, "lat", "lon")),
        check_vma=False,
    )
```

```python
import jax
import jax.numpy as jnp
from jax import lax
from jax.sharding import PartitionSpec as P
from jax.experimental import pallas as pl
from jax.experimental.pallas import tpu as pltpu
import functools

courant = 0.4
vert_mix = 0.1
rotation = 0.3
buoyancy = 0.3
bottom_drag = 0.2


SIXTIETH = 1.0 / 60.0
INTERPRET = False
CENTRAL = {-2: 1.0, -1: -8.0, 0: 37.0, 1: 37.0, 2: -8.0, 3: 1.0}
DAMPING = {-2: -1.0, -1: 5.0, 0: -10.0, 1: 10.0, 2: -5.0, 3: 1.0}


def shifted(x, step, axis):
    n = x.shape[axis]
    step = step % n
    if step == 0:
        return x
    return pltpu.roll(x, n - step, axis)


def wet_of(depth, k):
    return jnp.where(depth > k + 0.5, 1.0, 0.0)


def bottom_of(depth, k):
    return jnp.where(jnp.abs(depth - (k + 1.0)) < 0.5, 1.0, 0.0)


def face_terms(q, axis):
    m2 = shifted(q, -2, axis)
    m1 = shifted(q, -1, axis)
    p1 = shifted(q, 1, axis)
    p2 = shifted(q, 2, axis)
    p3 = shifted(q, 3, axis)
    central = 37.0 * (q + p1) - 8.0 * (m1 + p2) + (m2 + p3)
    damping = 10.0 * (p1 - q) - 5.0 * (p2 - m1) + (p3 - m2)
    return central, damping


def face_speed(wet, speed, axis):
    open_face = wet * shifted(wet, 1, axis)
    w = 0.5 * (speed + shifted(speed, 1, axis))
    s = jnp.sqrt(w * w + 0.0001)
    return open_face, w, s


def forward(src, store, depth, cor, terms, faces):
    level_count = src.shape[1]
    column = None
    for k in range(level_count):
        wet = wet_of(depth, k)
        bottom = bottom_of(depth, k)
        q = [src[f, k] for f in range(4)]
        density = (-0.2 * q[0] + 0.8 * q[1]) * wet
        column = density if column is None else column + density
        pressure = buoyancy * column
        div = [None] * 4
        for d, (axis, speed) in enumerate(((1, q[2]), (0, q[3]))):
            open_face, w, s = face_speed(wet, speed, axis)
            ratio = w / s
            w = w * SIXTIETH
            s = s * SIXTIETH
            faces[d, k, 0] = open_face
            faces[d, k, 1] = w
            faces[d, k, 2] = s
            for f in range(4):
                central, damping = face_terms(q[f], axis)
                terms[d, f, k] = central - ratio * damping
                flux = open_face * (w * central - s * damping)
                part = flux - shifted(flux, -1, axis)
                div[f] = part if div[f] is None else div[f] + part
        press_east = 0.5 * (shifted(pressure, 1, 1) - shifted(pressure, -1, 1))
        press_north = 0.5 * (shifted(pressure, 1, 0) - shifted(pressure, -1, 0))
        force = [
            None,
            None,
            cor * q[3] - press_east - bottom_drag * bottom * q[2],
            -cor * q[2] - press_north - bottom_drag * bottom * q[3],
        ]
        for f in range(4):
            vertical = None
            if k > 0:
                vertical = wet_of(depth, k - 1) * (src[f, k - 1] - q[f])
            if k < level_count - 1:
                below = wet_of(depth, k + 1) * (src[f, k + 1] - q[f])
                vertical = below if vertical is None else vertical + below
            value = q[f] - courant * div[f] + vert_mix * vertical
            if force[f] is not None:
                value = value + force[f]
            store(f, k, value * wet)


def backward(x, lam, store, g_ref, depth, cor, terms, faces):
    level_count = x.shape[1]
    for k in range(level_count):
        wet = wet_of(depth, k)
        for f in range(4):
            g_ref[f, k] = wet * lam[f, k]
    density_bar = [None] * level_count
    column = None
    for k in reversed(range(level_count)):
        gu = g_ref[2, k]
        gv = g_ref[3, k]
        pbar = 0.5 * (shifted(gu, 1, 1) - shifted(gu, -1, 1)) + 0.5 * (
            shifted(gv, 1, 0) - shifted(gv, -1, 0)
        )
        column = pbar if column is None else column + pbar
        density_bar[k] = buoyancy * column
    for k in range(level_count):
        wet = wet_of(depth, k)
        bottom = bottom_of(depth, k)
        q = [x[f, k] for f in range(4)]
        g = [g_ref[f, k] for f in range(4)]
        acc = list(g)
        for f in range(4):
            vertical = None
            if k > 0:
                vertical = wet * g_ref[f, k - 1] - wet_of(depth, k - 1) * g[f]
            if k < level_count - 1:
                below = wet * g_ref[f, k + 1] - wet_of(depth, k + 1) * g[f]
                vertical = below if vertical is None else vertical + below
            acc[f] = acc[f] + vert_mix * vertical
        acc[2] = acc[2] - bottom_drag * bottom * g[2] - cor * g[3]
        acc[3] = acc[3] + cor * g[2] - bottom_drag * bottom * g[3]
        acc[0] = acc[0] - 0.2 * wet * density_bar[k]
        acc[1] = acc[1] + 0.8 * wet * density_bar[k]
        for d, (axis, speed_field) in enumerate(((1, 2), (0, 3))):
            open_face = faces[d, k, 0]
            w = faces[d, k, 1]
            s = faces[d, k, 2]
            w_bar = None
            for f in range(4):
                flux_bar = (-courant * open_face) * (g[f] - shifted(g[f], 1, axis))
                part = flux_bar * terms[d, f, k]
                w_bar = part if w_bar is None else w_bar + part
                alpha = flux_bar * w
                beta = -flux_bar * s
                for j in range(-2, 4):
                    acc[f] = acc[f] + shifted(CENTRAL[j] * alpha + DAMPING[j] * beta, -j, axis)
            acc[speed_field] = acc[speed_field] + (0.5 * SIXTIETH) * (w_bar + shifted(w_bar, -1, axis))
        for f in range(4):
            store(f, k, acc[f])


def strip_place(p):
    return p // 10, 12 * (p % 10)


def assemble(dst, own, south, north, east, west, p, rowmask):
    rows, cols = own.shape
    depth = south.shape[0]
    frame_rows = dst.shape[0]
    dst[...] = jnp.zeros(dst.shape, jnp.float32)
    dst[0:rows, 0:cols] = own
    dst[rows : rows + depth, 0:cols] = south
    dst[frame_rows - depth : frame_rows, 0:cols] = north
    lane = lax.broadcasted_iota(jnp.int32, (frame_rows, 128), 1)
    block, offset = strip_place(p)
    from_east = shifted(east[:, 128 * block : 128 * (block + 1)], offset, 1)
    from_west = shifted(west[:, 128 * block : 128 * (block + 1)], offset - 116, 1)
    dst[:, cols : cols + 128] = jnp.where(lane < 12, from_east, jnp.where(lane >= 116, from_west, 0.0))
    dst[...] = dst[...] * rowmask


def two_step_kernel(
    margin, reach, own_x, own_c, own_d, north, south, west, east, rowmask_ref, cor_ref,
    final_ref, grad_ref, x0, lam, x1, mu, g_ref, depth_ref, terms_first, terms_second,
    faces_first, faces_second,
):
    fields, level_count, rows, cols = own_x.shape
    planes = fields * level_count
    frame_rows = x0.shape[2]
    rowmask = jnp.broadcast_to(rowmask_ref[...], (frame_rows, x0.shape[3]))
    cor = jnp.broadcast_to(cor_ref[...], (frame_rows, x0.shape[3]))
    east_msg = east[...]
    west_msg = west[...]
    for f in range(fields):
        for k in range(level_count):
            p = f * level_count + k
            assemble(
                x0.at[f, k], own_x[f, k], south[margin * p : margin * (p + 1), :],
                north[margin * p : margin * (p + 1), :], east_msg, west_msg, p, rowmask,
            )
    assemble(
        depth_ref, own_d[...], south[margin * planes : margin * (planes + 1), :],
        north[margin * planes : margin * (planes + 1), :], east_msg, west_msg, planes, rowmask,
    )
    base = margin * (planes + 1)
    for f in range(fields):
        for k in range(level_count):
            p = f * level_count + k
            assemble(
                lam.at[f, k], own_c[f, k], south[base + reach * p : base + reach * (p + 1), :],
                north[base + reach * p : base + reach * (p + 1), :], east_msg, west_msg,
                planes + 1 + p, rowmask,
            )
    depth = depth_ref[...]

    def keep(ref):
        def put(f, k, value):
            ref[f, k] = value
        return put

    def keep_cropped(ref):
        def put(f, k, value):
            ref[f, k] = value[:rows, :cols]
        return put

    forward(x0, keep(x1), depth, cor, terms_first, faces_first)
    forward(x1, keep_cropped(final_ref), depth, cor, terms_second, faces_second)
    backward(x1, lam, keep(mu), g_ref, depth, cor, terms_second, faces_second)
    backward(x0, mu, keep_cropped(grad_ref), g_ref, depth, cor, terms_first, faces_first)


def lat_pack_kernel(margin, reach, own_x, own_c, sea_ref, level_ref, north_msg, south_msg, own_d):
    fields, level_count, rows, cols = own_x.shape
    own_d[...] = (sea_ref[...] * level_ref[...]).astype(jnp.float32)
    planes = fields * level_count
    for f in range(fields):
        for k in range(level_count):
            p = f * level_count + k
            north_msg[margin * p : margin * (p + 1), :] = own_x[f, k, rows - margin : rows, :]
            south_msg[margin * p : margin * (p + 1), :] = own_x[f, k, 0:margin, :]
    north_msg[margin * planes : margin * (planes + 1), :] = own_d[rows - margin : rows, :]
    south_msg[margin * planes : margin * (planes + 1), :] = own_d[0:margin, :]
    base = margin * (planes + 1)
    for f in range(fields):
        for k in range(level_count):
            p = f * level_count + k
            north_msg[base + reach * p : base + reach * (p + 1), :] = own_c[f, k, rows - reach : rows, :]
            south_msg[base + reach * p : base + reach * (p + 1), :] = own_c[f, k, 0:reach, :]


def lon_strips(west_acc, east_acc, lane, p, ext_value):
    cols = ext_value.shape[1]
    block, offset = strip_place(p)
    keep = (lane >= offset) & (lane < offset + 12)
    last = shifted(ext_value[:, cols - 128 : cols], 116 - offset, 1)
    first = shifted(ext_value[:, 0:128], -offset, 1)
    west_acc[block] = west_acc[block] + jnp.where(keep, last, 0.0)
    east_acc[block] = east_acc[block] + jnp.where(keep, first, 0.0)


def lon_pack_own_kernel(own_x, own_c, own_d, west_msg, east_msg):
    fields, level_count, rows, cols = own_x.shape
    planes = fields * level_count
    lane = lax.broadcasted_iota(jnp.int32, (rows, 128), 1)
    blocks = west_msg.shape[1] // 128
    west_acc = [jnp.zeros((rows, 128), jnp.float32) for _ in range(blocks)]
    east_acc = [jnp.zeros((rows, 128), jnp.float32) for _ in range(blocks)]
    for f in range(fields):
        for k in range(level_count):
            p = f * level_count + k
            lon_strips(west_acc, east_acc, lane, p, own_x[f, k])
            lon_strips(west_acc, east_acc, lane, planes + 1 + p, own_c[f, k])
    lon_strips(west_acc, east_acc, lane, planes, own_d[...])
    for block in range(blocks):
        west_msg[:, 128 * block : 128 * (block + 1)] = west_acc[block]
        east_msg[:, 128 * block : 128 * (block + 1)] = east_acc[block]


def lon_pack_halo_kernel(margin, reach, west_own, east_own, north, south, west_msg, east_msg, ext):
    rows = west_own.shape[0]
    planes = (north.shape[0] - margin) // (margin + reach)
    halo_rows = ext.shape[0]
    lane = lax.broadcasted_iota(jnp.int32, (halo_rows, 128), 1)
    blocks = west_msg.shape[1] // 128
    west_acc = [jnp.zeros((halo_rows, 128), jnp.float32) for _ in range(blocks)]
    east_acc = [jnp.zeros((halo_rows, 128), jnp.float32) for _ in range(blocks)]

    def add_plane(p, south_rows, north_rows):
        depth = south_rows.shape[0]
        ext[...] = jnp.zeros(ext.shape, jnp.float32)
        ext[0:depth, :] = south_rows
        ext[halo_rows - depth : halo_rows, :] = north_rows
        lon_strips(west_acc, east_acc, lane, p, ext[...])

    for p in range(planes + 1):
        add_plane(p, south[margin * p : margin * (p + 1), :], north[margin * p : margin * (p + 1), :])
    base = margin * (planes + 1)
    for p in range(planes):
        add_plane(
            planes + 1 + p, south[base + reach * p : base + reach * (p + 1), :],
            north[base + reach * p : base + reach * (p + 1), :],
        )
    west_msg[0:rows, :] = west_own[...]
    east_msg[0:rows, :] = east_own[...]
    for block in range(blocks):
        west_msg[rows:, 128 * block : 128 * (block + 1)] = west_acc[block]
        east_msg[rows:, 128 * block : 128 * (block + 1)] = east_acc[block]


def ring(count, step):
    return [(i, (i + step) % count) for i in range(count)]


def shards(state, cotangent, seamask, levels):
    fields, level_count, row_count, col_count = state.shape
    lat_total = row_count * lax.axis_size("lat")
    lat_start = lax.axis_index("lat") * row_count
    margin = 12
    reach = 6
    rim = 10
    planes = fields * level_count
    vmem = pl.BlockSpec(memory_space=pltpu.VMEM)
    msg_rows = (planes + 1) * rim + planes * reach
    lat_msg = jax.ShapeDtypeStruct((msg_rows, col_count), jnp.float32)
    north_out, south_out, depth = pl.pallas_call(
        functools.partial(lat_pack_kernel, rim, reach),
        out_shape=(lat_msg, lat_msg, jax.ShapeDtypeStruct((row_count, col_count), jnp.float32)),
        in_specs=[vmem] * 4,
        out_specs=(vmem, vmem, vmem),
        interpret=INTERPRET,
    )(state, cotangent, seamask, levels)
    lat_count = lax.axis_size("lat")
    north = lax.ppermute(north_out, "lat", ring(lat_count, 1))
    south = lax.ppermute(south_out, "lat", ring(lat_count, -1))
    frame_rows = row_count + 2 * margin
    frame_cols = -(-(col_count + 2 * margin) // 128) * 128
    msg_cols = 128 * (-(-(2 * planes + 1) // 10))
    lon_msg = jax.ShapeDtypeStruct((frame_rows, msg_cols), jnp.float32)
    own_msg = jax.ShapeDtypeStruct((row_count, msg_cols), jnp.float32)
    west_own, east_own = pl.pallas_call(
        lon_pack_own_kernel,
        out_shape=(own_msg, own_msg),
        in_specs=[vmem] * 3,
        out_specs=(vmem, vmem),
        interpret=INTERPRET,
    )(state, cotangent, depth)
    west_out, east_out = pl.pallas_call(
        functools.partial(lon_pack_halo_kernel, rim, reach),
        out_shape=(lon_msg, lon_msg),
        in_specs=[vmem] * 4,
        out_specs=(vmem, vmem),
        scratch_shapes=[pltpu.VMEM((frame_rows - row_count, col_count), jnp.float32)],
        interpret=INTERPRET,
    )(west_own, east_own, north, south)
    lon_count = lax.axis_size("lon")
    west = lax.ppermute(west_out, "lon", ring(lon_count, 1))
    east = lax.ppermute(east_out, "lon", ring(lon_count, -1))
    frame_index = jnp.arange(frame_rows, dtype=jnp.int32)
    global_row = lat_start + jnp.where(frame_index < row_count + margin, frame_index, frame_index - frame_rows)
    rowmask = ((global_row >= 0) & (global_row < lat_total)).astype(jnp.float32)[:, None]
    latitude = jnp.pi * ((global_row.astype(jnp.float32) + 0.5) / lat_total - 0.5)
    cor = (rotation * jnp.sin(latitude))[:, None]
    frame = (fields, level_count, frame_rows, frame_cols)
    out_block = jax.ShapeDtypeStruct((fields, level_count, row_count, col_count), jnp.float32)
    final_state, adjoint_state = pl.pallas_call(
        functools.partial(two_step_kernel, rim, reach),
        out_shape=(out_block, out_block),
        in_specs=[vmem] * 9,
        out_specs=(vmem, vmem),
        scratch_shapes=[pltpu.VMEM(frame, jnp.float32) for _ in range(5)]
        + [pltpu.VMEM((frame_rows, frame_cols), jnp.float32)]
        + [pltpu.VMEM((2,) + frame, jnp.float32) for _ in range(2)]
        + [pltpu.VMEM((2, level_count, 3, frame_rows, frame_cols), jnp.float32) for _ in range(2)],
        interpret=INTERPRET,
    )(state, cotangent, depth, north, south, west, east, rowmask, cor)
    return (final_state, adjoint_state)


def solution(mesh):
    placed = (
        P(None, None, "lat", "lon"),
        P(None, None, "lat", "lon"),
        P("lat", "lon"),
        P("lat", "lon"),
    )
    return jax.shard_map(
        shards,
        mesh=mesh,
        in_specs=placed,
        out_specs=(P(None, None, "lat", "lon"), P(None, None, "lat", "lon")),
        check_vma=False,
    )
```
